256 devices in a mesh: group: 8 (over y, core), dev: 32 (over x, z).
Axes of the slice: x: 4, y: 4, z: 8, core: 2. Of those that a mesh axis runs over, the one named last changes fastest.
Arguments:
- embeddings: bfloat16 [262144, 768], P(('group', 'dev')), may hold values from -6 to 6
- cluster_ids: int32 [1024], P(('group', 'dev')), may hold values from 0 to 1023, as said below
Outputs:
- nearest: float32 [262144], P(('group', 'dev'))
The draws below stay inside these ranges and needn't reach their ends.
Inputs may be any that keep to these rules, and one draw needn't show every extreme that they name: `cluster_ids`: each cluster is a run of 1 to 29 consecutive blocks inside one cluster group of 128 blocks (a group's first block starts a cluster, its last block is a cluster of one block), and its id is the index of its first block; some cluster of every group has exactly 29 blocks.
All inputs are finite; a program needn't handle non-finite values.
Results may differ from the reference program's by a relative error of at most 0.0012.
Values may be sent and summed in bfloat16 or wider, within the bound.
No kernel may reach another device: no remote copies, remote signals or barrier semaphores. Data moves between devices by JAX's collectives and lax.ppermute only.
A program may use at most 192 MiB of HBM per device.

```python
import jax
import jax.numpy as jnp
from jax import lax

D = 768
BLK = 256
BPD = 4
CSPAN = 8
GBLK = 128
NBLK = 1024
ROWS = 262144
MOSTB = 29
N_GROUP = 8


def group_firsts(key, group):
    key_len, key_pos = jax.random.split(key)
    lengths = jax.random.randint(key_len, (GBLK,), 1, MOSTB + 1).astype(jnp.int32)
    slot = jnp.arange(GBLK, dtype=jnp.int32)
    where_big = jax.random.randint(key_pos, (), 0, 2).astype(jnp.int32)
    lengths = jnp.where(slot == where_big, MOSTB, lengths)
    starts = jnp.cumsum(lengths) - lengths
    begun = starts[None, :] <= slot[:, None]
    latest = jnp.max(jnp.where(begun, starts[None, :], 0), axis=1)
    latest = jnp.where(slot == GBLK - 1, GBLK - 1, latest)
    return (latest + group * GBLK).astype(jnp.int32)


def draw_cluster_ids(key, part):
    keys = jax.random.split(key, N_GROUP)
    firsts = jax.vmap(group_firsts)(keys, jnp.arange(N_GROUP, dtype=jnp.int32))
    return firsts.reshape(-1).astype(jnp.int32)


def level_of(key, shape, cuts, smallest, top_value):
    def one(position, parts):
        steps = jax.random.uniform(jax.random.fold_in(jax.random.fold_in(key, 6), position), (parts,), jnp.float32, smallest / len(cuts), top_value / len(cuts))
        return jnp.repeat(jnp.exp(steps), shape[position] // parts).reshape((-1,) + (1,) * (len(shape) - position - 1))

    level = one(*cuts[0])
    for cut in cuts[1:]:
        level = level * one(*cut)
    return level


def normal_values(own_key, extent, deviation, most, cuts=(), kind=jnp.bfloat16):
    entries = jax.random.normal(own_key, extent, jnp.float32) * deviation
    if len(cuts) > 0:
        entries = level_of(own_key, extent, cuts, -0.22, 0.18) * entries
    return jnp.clip(entries, min=-most, max=most).astype(kind)


def setup_inputs(seed: int = 0) -> dict:
    key_of = jax.random.split(jax.random.key(seed), 3)
    embeddings = normal_values(key_of[0], (ROWS, D), 1.0, 6.0, ((0, 256),))
    cluster_ids = draw_cluster_ids(jax.random.fold_in(key_of[2], 71), 0)
    return {"embeddings": embeddings, "cluster_ids": cluster_ids}


def reference(embeddings, cluster_ids):
    values_f = embeddings.astype(jnp.float32)
    squares = lax.optimization_barrier(jnp.sum(values_f * values_f, axis=1, keepdims=True))
    unit = (values_f * lax.rsqrt(squares + 1e-06)).astype(jnp.bfloat16)
    piece = BPD * BLK
    window = CSPAN * piece
    total = NBLK * BLK
    row_tags = jnp.repeat(cluster_ids + 1, BLK).astype(jnp.int32)
    padded_units = jnp.concatenate([unit, jnp.zeros((window, D), jnp.bfloat16)], axis=0)
    padded_tags = jnp.concatenate([row_tags, jnp.zeros((window,), jnp.int32)], axis=0)
    own_index = jnp.arange(piece, dtype=jnp.int32)
    near_index = jnp.arange(window, dtype=jnp.int32)

    def visit(carry, index):
        start = (index * piece).astype(jnp.int32)
        own = lax.dynamic_slice_in_dim(unit, start, piece, 0)
        own_tags = lax.dynamic_slice_in_dim(row_tags, start, piece, 0)
        near = lax.dynamic_slice_in_dim(padded_units, start, window, 0)
        near_tags = lax.dynamic_slice_in_dim(padded_tags, start, window, 0)
        scores = jnp.dot(own, near.T, preferred_element_type=jnp.float32)
        keep = (own_tags[:, None] == near_tags[None, :]) & (own_index[:, None] != near_index[None, :])
        shifted = jnp.where(keep, scores + 2.0, jnp.zeros_like(scores))
        part = lax.dynamic_slice_in_dim(carry, start, window, 0)
        carry = lax.dynamic_update_slice_in_dim(carry, jnp.maximum(part, lax.optimization_barrier(jnp.max(shifted, axis=0))), start, 0)
        return (carry, lax.optimization_barrier(jnp.max(shifted, axis=1)))
    carry_start = jnp.zeros((total + window,), jnp.float32)
    carry, row_best = lax.scan(visit, carry_start, jnp.arange(NBLK // BPD, dtype=jnp.int32))
    return jnp.maximum(row_best.reshape(-1), carry[:total]) - 2.0
```

```python
import jax
import jax.numpy as jnp
from jax import lax
from jax.sharding import PartitionSpec as P


def from_behind(value, axis, steps):
    count = lax.axis_size(axis)
    initial, last = (max(0, -steps), min(count, count - steps))
    return lax.ppermute(value, axis, [(source, source + steps) for source in range(initial, last)])


def unit_rows(embeddings):
    values_f = embeddings.astype(jnp.float32)
    squares = jnp.sum(values_f * values_f, axis=1, keepdims=True)
    return (values_f * lax.rsqrt(squares + 1e-06)).astype(jnp.bfloat16)


def body(embeddings, cluster_ids):
    rows = embeddings.shape[0]
    blocks = cluster_ids.shape[0]
    width = rows // blocks
    count = lax.axis_size("dev")
    reach = count // 4
    place = lax.axis_index("dev")
    unit = unit_rows(embeddings)
    all_tags = lax.all_gather(cluster_ids, "dev", tiled=True) + 1

    def tags_at(offset, sentinel):
        index = place + offset
        valid = (index >= 0) & (index < count)
        start = jnp.clip(index, 0, count - 1) * blocks
        tags = lax.dynamic_slice_in_dim(all_tags, start, blocks, 0)
        return jnp.repeat(jnp.where(valid, tags, sentinel), width)

    def tile(a, a_tags, b, b_tags):
        sims = jnp.dot(a, b.T, preferred_element_type=jnp.float32)
        shifted = jnp.where(a_tags[:, None] == b_tags[None, :], sims + 2.0, jnp.zeros_like(sims))
        return jnp.max(shifted, axis=1), jnp.max(shifted, axis=0)

    own_tags = jnp.repeat(cluster_ids + 1, width)
    local = jnp.arange(rows, dtype=jnp.int32)
    scores = jnp.dot(unit, unit.T, preferred_element_type=jnp.float32)
    keep = (own_tags[:, None] == own_tags[None, :]) & (local[:, None] != local[None, :])
    best = jnp.max(jnp.where(keep, scores + 2.0, jnp.zeros_like(scores)), axis=1)

    ahead_steps = reach // 2
    behind_steps = (reach - 1) // 2
    ahead = [unit]
    for step in range(ahead_steps):
        ahead.append(from_behind(ahead[-1], "dev", -1))
    behind = [unit]
    for step in range(behind_steps):
        behind.append(from_behind(behind[-1], "dev", 1))
    ahead_tags = [own_tags] + [tags_at(j, -2) for j in range(1, ahead_steps + 1)]
    behind_tags = [own_tags] + [tags_at(-i, -1) for i in range(1, behind_steps + 1)]

    to_ahead = [None] * (ahead_steps + 1)
    to_behind = [None] * (behind_steps + 1)
    for k in range(1, reach):
        i, j = k // 2, k - k // 2
        row_part, column_part = tile(behind[i], behind_tags[i], ahead[j], ahead_tags[j])
        if i == 0:
            best = jnp.maximum(best, row_part)
        else:
            to_behind[i] = row_part if to_behind[i] is None else jnp.maximum(to_behind[i], row_part)
        to_ahead[j] = column_part if to_ahead[j] is None else jnp.maximum(to_ahead[j], column_part)

    for i in range(1, behind_steps + 1):
        best = jnp.maximum(best, from_behind(to_behind[i], "dev", -i))
    for j in range(1, ahead_steps + 1):
        best = jnp.maximum(best, from_behind(to_ahead[j], "dev", j))
    return best - 2.0


def solution(mesh):
    return jax.shard_map(
        body,
        mesh=mesh,
        in_specs=(P(("group", "dev"), None), P(("group", "dev"))),
        out_specs=P(("group", "dev")),
        check_vma=False,
    )
```

```python
import jax
import jax.numpy as jnp
from jax import lax
from jax.sharding import PartitionSpec as P


def from_behind(value, axis, steps):
    count = lax.axis_size(axis)
    initial, last = (max(0, -steps), min(count, count - steps))
    return lax.ppermute(value, axis, [(source, source + steps) for source in range(initial, last)])


def unit_rows(embeddings):
    values_f = embeddings.astype(jnp.float32)
    squares = jnp.sum(values_f * values_f, axis=1, keepdims=True)
    return (values_f * lax.rsqrt(squares + 1e-06)).astype(jnp.bfloat16)


def body(embeddings, cluster_ids):
    rows = embeddings.shape[0]
    blocks = cluster_ids.shape[0]
    width = rows // blocks
    count = lax.axis_size("dev")
    reach = count // 4
    place = lax.axis_index("dev")
    first_block = (lax.axis_index("group") * count + place) * blocks
    unit = unit_rows(embeddings)

    own_tags = jnp.repeat(cluster_ids + 1, width)
    local = jnp.arange(rows, dtype=jnp.int32)
    scores = jnp.dot(unit, unit.T, preferred_element_type=jnp.float32)
    keep = (own_tags[:, None] == own_tags[None, :]) & (local[:, None] != local[None, :])
    best = jnp.max(jnp.where(keep, scores + 2.0, jnp.zeros_like(scores)), axis=1)

    ahead_steps = reach // 2
    behind_steps = (reach - 1) // 2
    ahead = [unit]
    for step in range(ahead_steps):
        ahead.append(from_behind(ahead[-1], "dev", -1))
    behind = [unit]
    for step in range(behind_steps):
        behind.append(from_behind(behind[-1], "dev", 1))
    ahead_ids = [cluster_ids] + [from_behind(cluster_ids, "dev", -j) for j in range(1, ahead_steps + 1)]

    def tile(i, j):
        a, b = behind[i], ahead[j]
        a_blocks = first_block - i * blocks + jnp.arange(blocks, dtype=jnp.int32)
        valid = place + j < count
        block_same = (ahead_ids[j][None, :] <= a_blocks[:, None]) & valid
        matched = jnp.any(block_same)

        def compute(unused):
            sims = jnp.dot(a, b.T, preferred_element_type=jnp.float32)
            same = jnp.repeat(jnp.repeat(block_same, width, axis=0), width, axis=1)
            shifted = jnp.where(same, sims + 2.0, jnp.zeros_like(sims))
            return jnp.max(shifted, axis=1), jnp.max(shifted, axis=0)

        def skipped(unused):
            empty = jnp.zeros((rows,), jnp.float32)
            return (empty, empty)

        return lax.cond(matched, compute, skipped, 0)

    to_ahead = [None] * (ahead_steps + 1)
    to_behind = [None] * (behind_steps + 1)
    for k in range(1, reach):
        i, j = k // 2, k - k // 2
        row_part, column_part = tile(i, j)
        if i == 0:
            best = jnp.maximum(best, row_part)
        else:
            to_behind[i] = row_part if to_behind[i] is None else jnp.maximum(to_behind[i], row_part)
        to_ahead[j] = column_part if to_ahead[j] is None else jnp.maximum(to_ahead[j], column_part)

    for i in range(1, behind_steps + 1):
        best = jnp.maximum(best, from_behind(to_behind[i], "dev", -i))
    for j in range(1, ahead_steps + 1):
        best = jnp.maximum(best, from_behind(to_ahead[j], "dev", j))
    return best - 2.0


def solution(mesh):
    return jax.shard_map(
        body,
        mesh=mesh,
        in_specs=(P(("group", "dev"), None), P(("group", "dev"))),
        out_specs=P(("group", "dev")),
        check_vma=False,
    )
```

```python
import jax
import jax.numpy as jnp
from jax import lax
from jax.sharding import PartitionSpec as P


def from_behind(value, axis, steps):
    count = lax.axis_size(axis)
    initial, last = (max(0, -steps), min(count, count - steps))
    return lax.ppermute(value, axis, [(source, source + steps) for source in range(initial, last)])


def unit_rows(embeddings):
    values_f = embeddings.astype(jnp.float32)
    squares = jnp.sum(values_f * values_f, axis=1, keepdims=True)
    return (values_f * lax.rsqrt(squares + 1e-06)).astype(jnp.bfloat16)


def body(embeddings, cluster_ids):
    rows, dim = embeddings.shape
    blocks = cluster_ids.shape[0]
    width = rows // blocks
    half = blocks // 2
    count = lax.axis_size("dev")
    place = lax.axis_index("dev")
    first_block = (lax.axis_index("group") * count + place) * blocks
    unit = unit_rows(embeddings)

    own_tags = jnp.repeat(cluster_ids, width)
    local = jnp.arange(rows, dtype=jnp.int32)
    scores = jnp.dot(unit, unit.T, preferred_element_type=jnp.float32)
    keep = (own_tags[:, None] == own_tags[None, :]) & (local[:, None] != local[None, :])
    best = jnp.max(jnp.where(keep, scores + 2.0, jnp.zeros_like(scores)), axis=1)

    lag = first_block + jnp.arange(blocks, dtype=jnp.int32) - cluster_ids
    meta = jnp.zeros((16, dim), jnp.bfloat16).at[0, :blocks].set(lag.astype(jnp.bfloat16))
    packet = jnp.concatenate([unit, meta], axis=0)

    ahead = [packet]
    for step in range(3):
        ahead.append(from_behind(ahead[-1], "dev", -1))
    ahead.append(from_behind(jnp.concatenate([ahead[3][: half * width], ahead[3][rows:]], axis=0), "dev", -1))
    behind = [unit]
    for step in range(3):
        behind.append(from_behind(behind[-1], "dev", 1))
    behind.append(from_behind(behind[3][half * width:], "dev", 1))

    def tile(i, a_blocks, j, b_count):
        a = behind[i]
        b = ahead[j][: b_count * width]
        b_lag = ahead[j][b_count * width, :b_count].astype(jnp.int32)
        gap = (i + j) * blocks + jnp.arange(b_count, dtype=jnp.int32)[None, :] - jnp.array(a_blocks, jnp.int32)[:, None]
        block_same = (gap <= b_lag[None, :]) & (place >= i)
        matched = jnp.any(block_same)

        def compute(unused):
            sims = jnp.dot(a, b.T, preferred_element_type=jnp.float32)
            same = jnp.repeat(jnp.repeat(block_same, width, axis=0), width, axis=1)
            shifted = jnp.where(same, sims + 2.0, jnp.zeros_like(sims))
            return jnp.max(shifted, axis=1), jnp.max(shifted, axis=0)

        def skipped(unused):
            return (jnp.zeros((a.shape[0],), jnp.float32), jnp.zeros((b.shape[0],), jnp.float32))

        return lax.cond(matched, compute, skipped, 0)

    everything = list(range(blocks))
    plan = [(k // 2, everything, k - k // 2, blocks) for k in range(1, 7)]
    plan += [(3, everything, 4, half), (4, everything[half:], 3, blocks)]
    to_ahead = {}
    to_behind = {}
    for i, a_blocks, j, b_count in plan:
        row_part, column_part = tile(i, a_blocks, j, b_count)
        if i == 0:
            best = jnp.maximum(best, row_part)
        else:
            to_behind[i] = jnp.maximum(to_behind[i], row_part) if i in to_behind else row_part
        to_ahead[j] = jnp.maximum(to_ahead[j], column_part) if j in to_ahead else column_part

    for i, part in to_behind.items():
        arrived = from_behind(part, "dev", -i)
        best = best.at[rows - part.shape[0]:].max(arrived)
    for j, part in to_ahead.items():
        arrived = from_behind(part, "dev", j)
        best = best.at[: part.shape[0]].max(arrived)
    return best - 2.0


def solution(mesh):
    return jax.shard_map(
        body,
        mesh=mesh,
        in_specs=(P(("group", "dev"), None), P(("group", "dev"))),
        out_specs=P(("group", "dev")),
        check_vma=False,
    )
```

```python
import jax
import jax.numpy as jnp
from jax import lax
from jax.sharding import PartitionSpec as P


def from_behind(value, axis, steps):
    count = lax.axis_size(axis)
    initial, last = (max(0, -steps), min(count, count - steps))
    return lax.ppermute(value, axis, [(source, source + steps) for source in range(initial, last)])


def unit_rows(embeddings):
    values_f = embeddings.astype(jnp.float32)
    squares = jnp.sum(values_f * values_f, axis=1, keepdims=True)
    return (values_f * lax.rsqrt(squares + 1e-06)).astype(jnp.bfloat16)


def body(embeddings, cluster_ids):
    rows, dim = embeddings.shape
    blocks = cluster_ids.shape[0]
    width = rows // blocks
    half = blocks // 2
    count = lax.axis_size("dev")
    place = lax.axis_index("dev")
    first_block = (lax.axis_index("group") * count + place) * blocks
    unit = unit_rows(embeddings)

    own_tags = jnp.repeat(cluster_ids, width)
    local = jnp.arange(rows, dtype=jnp.int32)
    scores = jnp.dot(unit, unit.T, preferred_element_type=jnp.float32)
    keep = (own_tags[:, None] == own_tags[None, :]) & (local[:, None] != local[None, :])
    best = jnp.max(jnp.where(keep, scores + 2.0, jnp.zeros_like(scores)), axis=1)

    lag = first_block + jnp.arange(blocks, dtype=jnp.int32) - cluster_ids
    meta = jnp.zeros((16, dim), jnp.bfloat16).at[0, :blocks].set(lag.astype(jnp.bfloat16))
    packet = jnp.concatenate([unit, meta], axis=0)

    ahead = [packet]
    for step in range(3):
        ahead.append(from_behind(ahead[-1], "dev", -1))
    ahead.append(from_behind(jnp.concatenate([ahead[3][: half * width], ahead[3][rows:]], axis=0), "dev", -1))
    behind = [unit]
    for step in range(3):
        behind.append(from_behind(behind[-1], "dev", 1))
    behind.append(from_behind(behind[3][half * width:], "dev", 1))

    def tile(i, a_blocks, j, b_count):
        a = behind[i]
        b = ahead[j]
        b_lag = b[b_count * width, :b_count].astype(jnp.int32)
        block_reach = (i + j) * blocks + jnp.arange(b_count, dtype=jnp.int32) - b_lag
        a_rows = jnp.repeat(jnp.array(a_blocks, jnp.int32), width)
        b_rows = jnp.concatenate(
            [jnp.repeat(block_reach, width), jnp.full((b.shape[0] - b_count * width,), rows, jnp.int32)]
        )
        matched = (jnp.min(block_reach) <= a_blocks[-1]) & (place >= i)

        def compute(unused):
            sims = jnp.dot(a, b.T, preferred_element_type=jnp.float32)
            same = b_rows[None, :] <= a_rows[:, None]
            shifted = jnp.where(same, sims + 2.0, jnp.zeros_like(sims))
            return jnp.max(shifted, axis=1), jnp.max(shifted, axis=0)[: b_count * width]

        def skipped(unused):
            return (jnp.zeros((a.shape[0],), jnp.float32), jnp.zeros((b_count * width,), jnp.float32))

        return lax.cond(matched, compute, skipped, 0)

    everything = list(range(blocks))
    plan = [(k // 2, everything, k - k // 2, blocks) for k in range(1, 7)]
    plan += [(3, everything, 4, half), (4, everything[half:], 3, blocks)]
    to_ahead = {}
    to_behind = {}
    for i, a_blocks, j, b_count in plan:
        row_part, column_part = tile(i, a_blocks, j, b_count)
        if i == 0:
            best = jnp.maximum(best, row_part)
        else:
            to_behind[i] = jnp.maximum(to_behind[i], row_part) if i in to_behind else row_part
        to_ahead[j] = jnp.maximum(to_ahead[j], column_part) if j in to_ahead else column_part

    for i, part in to_behind.items():
        arrived = from_behind(part, "dev", -i)
        best = best.at[rows - part.shape[0]:].max(arrived)
    for j, part in to_ahead.items():
        arrived = from_behind(part, "dev", j)
        best = best.at[: part.shape[0]].max(arrived)
    return best - 2.0


def solution(mesh):
    return jax.shard_map(
        body,
        mesh=mesh,
        in_specs=(P(("group", "dev"), None), P(("group", "dev"))),
        out_specs=P(("group", "dev")),
        check_vma=False,
    )
```

```python
import jax
import jax.numpy as jnp
from jax import lax
from jax.sharding import PartitionSpec as P


def from_behind(value, axis, steps):
    count = lax.axis_size(axis)
    initial, last = (max(0, -steps), min(count, count - steps))
    return lax.ppermute(value, axis, [(source, source + steps) for source in range(initial, last)])


def unit_rows(embeddings):
    values_f = embeddings.astype(jnp.float32)
    squares = jnp.sum(values_f * values_f, axis=1, keepdims=True)
    return (values_f * lax.rsqrt(squares + 1e-06)).astype(jnp.bfloat16)


def body(embeddings, cluster_ids):
    rows, dim = embeddings.shape
    blocks = cluster_ids.shape[0]
    width = rows // blocks
    half = blocks // 2
    count = lax.axis_size("dev")
    place = lax.axis_index("dev")
    first_block = (lax.axis_index("group") * count + place) * blocks
    unit = unit_rows(embeddings)

    own_tags = jnp.repeat(cluster_ids, width)
    local = jnp.arange(rows, dtype=jnp.int32)
    scores = jnp.dot(unit, unit.T, preferred_element_type=jnp.float32)
    keep = (own_tags[:, None] == own_tags[None, :]) & (local[:, None] != local[None, :])
    best = jnp.max(jnp.where(keep, scores + 2.0, jnp.zeros_like(scores)), axis=1)

    lag = first_block + jnp.arange(blocks, dtype=jnp.int32) - cluster_ids
    meta = jnp.zeros((16, dim), jnp.bfloat16).at[0, :blocks].set(lag.astype(jnp.bfloat16))
    packet = jnp.concatenate([unit, meta], axis=0)

    def tile(i, a_blocks, j, b_count):
        a = behind[i]
        b = ahead[j]
        b_lag = b[b_count * width, :b_count].astype(jnp.int32)
        block_reach = (i + j) * blocks + jnp.arange(b_count, dtype=jnp.int32) - b_lag
        a_rows = jnp.repeat(jnp.array(a_blocks, jnp.int32), width)
        b_rows = jnp.concatenate(
            [jnp.repeat(block_reach, width), jnp.full((b.shape[0] - b_count * width,), rows, jnp.int32)]
        )
        matched = (jnp.min(block_reach) <= a_blocks[-1]) & (place >= i)

        def compute(unused):
            sims = jnp.dot(a, b.T, preferred_element_type=jnp.float32)
            same = b_rows[None, :] <= a_rows[:, None]
            shifted = jnp.where(same, sims + 2.0, jnp.zeros_like(sims))
            return jnp.max(shifted, axis=1), jnp.max(shifted, axis=0)[: b_count * width]

        def skipped(unused):
            return (jnp.zeros((a.shape[0],), jnp.float32), jnp.zeros((b_count * width,), jnp.float32))

        return lax.cond(matched, compute, skipped, 0)

    everything = list(range(blocks))
    plan = [(k // 2, everything, k - k // 2, blocks) for k in range(1, 7)]
    plan += [(3, everything, 4, half), (4, everything[half:], 3, blocks)]
    to_ahead = {}
    to_behind = {}

    def gather(pieces):
        nonlocal best
        for (i, a_blocks, j, b_count), (row_part, column_part) in pieces:
            if i == 0:
                best = jnp.maximum(best, row_part)
            else:
                to_behind[i] = jnp.maximum(to_behind[i], row_part) if i in to_behind else row_part
            to_ahead[j] = jnp.maximum(to_ahead[j], column_part) if j in to_ahead else column_part

    ahead = [packet]
    behind = [unit]
    hops = 4
    for hop in range(1, hops + 1):
        if hop < hops:
            a_next = from_behind(ahead[-1], "dev", -1)
            b_next = from_behind(behind[-1], "dev", 1)
        else:
            a_next = from_behind(jnp.concatenate([ahead[-1][: half * width], ahead[-1][rows:]], axis=0), "dev", -1)
            b_next = from_behind(behind[-1][half * width:], "dev", 1)
        ready = [entry for entry in plan if max(entry[0], entry[2]) == hop - 1]
        pieces = [tile(*entry) for entry in ready]
        a_next, b_next, best, pieces = lax.optimization_barrier((a_next, b_next, best, pieces))
        gather(zip(ready, pieces))
        ahead.append(a_next)
        behind.append(b_next)
    ready = [entry for entry in plan if max(entry[0], entry[2]) == hops]
    gather(zip(ready, [tile(*entry) for entry in ready]))

    for i, part in to_behind.items():
        arrived = from_behind(part, "dev", -i)
        best = best.at[rows - part.shape[0]:].max(arrived)
    for j, part in to_ahead.items():
        arrived = from_behind(part, "dev", j)
        best = best.at[: part.shape[0]].max(arrived)
    return best - 2.0


def solution(mesh):
    return jax.shard_map(
        body,
        mesh=mesh,
        in_specs=(P(("group", "dev"), None), P(("group", "dev"))),
        out_specs=P(("group", "dev")),
        check_vma=False,
    )
```

```python
import jax
import jax.numpy as jnp
from jax import lax
from jax.sharding import PartitionSpec as P


def shift(value, axis, steps, cyclic=False):
    count = lax.axis_size(axis)
    if cyclic:
        pairs = [(source, (source + steps) % count) for source in range(count)]
    else:
        pairs = [(source, source + steps) for source in range(max(0, -steps), min(count, count - steps))]
    return lax.ppermute(value, axis, pairs)


def unit_rows(embeddings):
    values_f = embeddings.astype(jnp.float32)
    squares = jnp.sum(values_f * values_f, axis=1, keepdims=True)
    return (values_f * lax.rsqrt(squares + 1e-06)).astype(jnp.bfloat16)


def body(embeddings, cluster_ids):
    rows, dim = embeddings.shape
    blocks = cluster_ids.shape[0]
    width = rows // blocks
    half = blocks // 2
    count = lax.axis_size("dev")
    stride = count // 4
    place = lax.axis_index("dev")
    first_block = (lax.axis_index("group") * count + place) * blocks
    unit = unit_rows(embeddings)

    own_tags = jnp.repeat(cluster_ids, width)
    local = jnp.arange(rows, dtype=jnp.int32)
    scores = jnp.dot(unit, unit.T, preferred_element_type=jnp.float32)
    keep = (own_tags[:, None] == own_tags[None, :]) & (local[:, None] != local[None, :])
    best = jnp.max(jnp.where(keep, scores + 2.0, jnp.zeros_like(scores)), axis=1)

    lag = first_block + jnp.arange(blocks, dtype=jnp.int32) - cluster_ids
    meta = jnp.zeros((16, dim), jnp.bfloat16).at[0, :blocks].set(lag.astype(jnp.bfloat16))
    extra = meta.shape[0]
    packet = jnp.concatenate([unit, meta], axis=0)
    everything = tuple(range(blocks))
    low, high = everything[:half], everything[half:]

    def part(pk, chosen):
        return jnp.concatenate([pk[chosen[0] * width:(chosen[-1] + 1) * width], pk[-extra:]], axis=0)

    def tile(a, a_blocks, b, b_blocks, k, valid):
        nb = len(b_blocks)
        lags = b[nb * width, b_blocks[0]:b_blocks[-1] + 1].astype(jnp.int32)
        block_reach = k * blocks + jnp.array(b_blocks, jnp.int32) - lags
        a_rows = jnp.concatenate([
            jnp.repeat(jnp.array(a_blocks, jnp.int32), width),
            jnp.full((a.shape[0] - len(a_blocks) * width,), -4 * rows, jnp.int32)])
        b_rows = jnp.concatenate([
            jnp.repeat(block_reach, width),
            jnp.full((b.shape[0] - nb * width,), 4 * rows, jnp.int32)])
        matched = (jnp.min(block_reach) <= max(a_blocks)) & valid

        def compute(unused):
            sims = jnp.dot(a, b.T, preferred_element_type=jnp.float32)
            same = b_rows[None, :] <= a_rows[:, None]
            shifted = jnp.where(same, sims + 2.0, jnp.zeros_like(sims))
            return (jnp.max(shifted, axis=1)[: len(a_blocks) * width],
                    jnp.max(shifted, axis=0)[: nb * width])

        def skipped(unused):
            return (jnp.zeros((len(a_blocks) * width,), jnp.float32),
                    jnp.zeros((nb * width,), jnp.float32))

        return lax.cond(matched, compute, skipped, 0)

    far = shift(unit, "dev", stride, cyclic=True)
    far_ok = [(place >= stride) | (place < m) for m in range(4)]
    ahead = [packet]
    behind = [packet]
    def plan_of():
        return [
            (1, ("own",), everything, ("ahead", 1), everything, 1, True, ("best",), ("ahead", 1)),
            (1, ("behind", 1), everything, ("ahead", 1), everything, 2, place >= 1, ("behind", 1), ("ahead", 1)),
            (1, ("far",), everything, ("behind", 1), everything, stride - 1, far_ok[1], ("far",), ("behind", 1)),
            (2, ("behind", 1), everything, ("ahead", 2), everything, 3, place >= 1, ("behind", 1), ("ahead", 2)),
            (2, ("behind", 2), everything, ("ahead", 2), everything, 4, place >= 2, ("behind", 2), ("ahead", 2)),
            (2, ("far",), everything, ("behind", 2), everything, stride - 2, far_ok[2], ("far",), ("behind", 2)),
            (3, ("behind", 2), everything, ("ahead", 3), low, 5, place >= 2, ("behind", 2), ("ahead", 3)),
            (3, ("far",), everything, ("behind", 3), high, stride - 3, far_ok[3], ("far",), ("behind", 3)),
        ]

    def fetch(where):
        if where[0] == "own":
            return unit
        if where[0] == "far":
            return far
        return (ahead if where[0] == "ahead" else behind)[where[1]]

    sends = {}

    def gather(dest, chosen, value):
        nonlocal best
        if dest == ("best",):
            best = best.at[chosen[0] * width:(chosen[-1] + 1) * width].max(value)
        elif dest in sends:
            sends[dest] = (chosen, jnp.maximum(sends[dest][1], value))
        else:
            sends[dest] = (chosen, value)

    hops = 3
    plan = plan_of()
    for hop in range(1, hops + 1):
        if hop < hops:
            a_next = shift(ahead[-1], "dev", -1)
            b_next = shift(behind[-1], "dev", 1, cyclic=True)
        else:
            a_next = shift(part(ahead[-1], low), "dev", -1)
            b_next = shift(part(behind[-1], high), "dev", 1, cyclic=True)
        ready = [entry for entry in plan if entry[0] == hop - 1]
        pieces = [tile(fetch(e[1]), e[2], fetch(e[3]), e[4], e[5], e[6]) for e in ready]
        if hop == 1:
            a_next, b_next, far, best = lax.optimization_barrier((a_next, b_next, far, best))
        else:
            a_next, b_next, pieces = lax.optimization_barrier((a_next, b_next, pieces))
        for e, (row_part, column_part) in zip(ready, pieces):
            gather(e[7], e[2], row_part)
            gather(e[8], e[4], column_part)
        ahead.append(a_next)
        behind.append(b_next)
    ready = [entry for entry in plan if entry[0] == hops]
    for e in ready:
        row_part, column_part = tile(fetch(e[1]), e[2], fetch(e[3]), e[4], e[5], e[6])
        gather(e[7], e[2], row_part)
        gather(e[8], e[4], column_part)

    for dest, (chosen, value) in sends.items():
        if dest[0] == "ahead":
            arrived = shift(value, "dev", dest[1])
        elif dest[0] == "behind":
            arrived = shift(value, "dev", -dest[1], cyclic=True)
        else:
            arrived = shift(value, "dev", -stride, cyclic=True)
        best = best.at[chosen[0] * width:(chosen[-1] + 1) * width].max(arrived)
    return best - 2.0


def solution(mesh):
    return jax.shard_map(
        body,
        mesh=mesh,
        in_specs=(P(("group", "dev"), None), P(("group", "dev"))),
        out_specs=P(("group", "dev")),
        check_vma=False,
    )
```

```python
import jax
import jax.numpy as jnp
from jax import lax
from jax.sharding import PartitionSpec as P


def shift(value, axis, steps, cyclic=False):
    count = lax.axis_size(axis)
    if cyclic:
        pairs = [(source, (source + steps) % count) for source in range(count)]
    else:
        pairs = [(source, source + steps) for source in range(max(0, -steps), min(count, count - steps))]
    return lax.ppermute(value, axis, pairs)


def unit_rows(embeddings):
    values_f = embeddings.astype(jnp.float32)
    squares = jnp.sum(values_f * values_f, axis=1, keepdims=True)
    return (values_f * lax.rsqrt(squares + 1e-06)).astype(jnp.bfloat16)


def body(embeddings, cluster_ids):
    rows, dim = embeddings.shape
    blocks = cluster_ids.shape[0]
    width = rows // blocks
    half = blocks // 2
    count = lax.axis_size("dev")
    stride = count // 4
    place = lax.axis_index("dev")
    first_block = (lax.axis_index("group") * count + place) * blocks
    unit = unit_rows(embeddings)

    own_tags = jnp.repeat(cluster_ids, width)
    local = jnp.arange(rows, dtype=jnp.int32)
    scores = jnp.dot(unit, unit.T, preferred_element_type=jnp.float32)
    keep = (own_tags[:, None] == own_tags[None, :]) & (local[:, None] != local[None, :])
    best = jnp.max(jnp.where(keep, scores + 2.0, jnp.zeros_like(scores)), axis=1)

    lag = first_block + jnp.arange(blocks, dtype=jnp.int32) - cluster_ids
    meta = jnp.zeros((16, dim), jnp.bfloat16).at[0, :blocks].set(lag.astype(jnp.bfloat16))
    extra = meta.shape[0]
    packet = jnp.concatenate([unit, meta], axis=0)
    everything = tuple(range(blocks))
    low, high = everything[:half], everything[half:]

    def part(pk, chosen):
        return jnp.concatenate([pk[chosen[0] * width:(chosen[-1] + 1) * width], pk[-extra:]], axis=0)

    def tile(a, a_blocks, b, b_blocks, k, valid):
        nb = len(b_blocks)
        lags = b[nb * width, b_blocks[0]:b_blocks[-1] + 1].astype(jnp.int32)
        block_reach = k * blocks + jnp.array(b_blocks, jnp.int32) - lags
        a_rows = jnp.concatenate([
            jnp.repeat(jnp.array(a_blocks, jnp.int32), width),
            jnp.full((a.shape[0] - len(a_blocks) * width,), -4 * rows, jnp.int32)])
        b_rows = jnp.concatenate([
            jnp.repeat(block_reach, width),
            jnp.full((b.shape[0] - nb * width,), 4 * rows, jnp.int32)])
        matched = (jnp.min(block_reach) <= max(a_blocks)) & valid

        def compute(unused):
            sims = jnp.dot(a, b.T, preferred_element_type=jnp.float32)
            same = b_rows[None, :] <= a_rows[:, None]
            shifted = jnp.where(same, sims + 2.0, jnp.zeros_like(sims))
            return (jnp.max(shifted, axis=1)[: len(a_blocks) * width],
                    jnp.max(shifted, axis=0)[: nb * width])

        def skipped(unused):
            return (jnp.zeros((len(a_blocks) * width,), jnp.float32),
                    jnp.zeros((nb * width,), jnp.float32))

        return lax.cond(matched, compute, skipped, 0)

    far = shift(unit, "dev", stride, cyclic=True)
    far_ok = [(place >= stride) | (place < m) for m in range(4)]
    ahead = [packet]
    behind = [packet]
    def plan_of():
        return [
            (1, ("own",), everything, ("ahead", 1), everything, 1, True, ("best",), ("ahead", 1)),
            (1, ("behind", 1), everything, ("ahead", 1), everything, 2, place >= 1, ("behind", 1), ("ahead", 1)),
            (2, ("behind", 1), everything, ("ahead", 2), everything, 3, place >= 1, ("behind", 1), ("ahead", 2)),
            (2, ("behind", 2), everything, ("ahead", 2), everything, 4, place >= 2, ("behind", 2), ("ahead", 2)),
            (2, ("far",), everything, ("behind", 1), everything, stride - 1, far_ok[1], ("far",), ("behind", 1)),
            (2, ("far",), everything, ("behind", 2), everything, stride - 2, far_ok[2], ("far",), ("behind", 2)),
            (3, ("behind", 2), everything, ("ahead", 3), low, 5, place >= 2, ("behind", 2), ("ahead", 3)),
            (3, ("far",), everything, ("behind", 3), high, stride - 3, far_ok[3], ("far",), ("behind", 3)),
        ]

    def fetch(where):
        if where[0] == "own":
            return unit
        if where[0] == "far":
            return far
        return (ahead if where[0] == "ahead" else behind)[where[1]]

    sends = {}

    def gather(dest, chosen, value):
        nonlocal best
        if dest == ("best",):
            best = best.at[chosen[0] * width:(chosen[-1] + 1) * width].max(value)
        elif dest in sends:
            sends[dest] = (chosen, jnp.maximum(sends[dest][1], value))
        else:
            sends[dest] = (chosen, value)

    hops = 3
    plan = plan_of()
    for hop in range(1, hops + 1):
        if hop < hops:
            a_next = shift(ahead[-1], "dev", -1)
            b_next = shift(behind[-1], "dev", 1, cyclic=True)
        else:
            a_next = shift(part(ahead[-1], low), "dev", -1)
            b_next = shift(part(behind[-1], high), "dev", 1, cyclic=True)
        ready = [entry for entry in plan if entry[0] == hop - 1]
        pieces = [tile(fetch(e[1]), e[2], fetch(e[3]), e[4], e[5], e[6]) for e in ready]
        if hop == 1:
            a_next, b_next, best = lax.optimization_barrier((a_next, b_next, best))
        else:
            a_next, b_next, pieces = lax.optimization_barrier((a_next, b_next, pieces))
        for e, (row_part, column_part) in zip(ready, pieces):
            gather(e[7], e[2], row_part)
            gather(e[8], e[4], column_part)
        ahead.append(a_next)
        behind.append(b_next)
    ready = [entry for entry in plan if entry[0] == hops]
    for e in ready:
        row_part, column_part = tile(fetch(e[1]), e[2], fetch(e[3]), e[4], e[5], e[6])
        gather(e[7], e[2], row_part)
        gather(e[8], e[4], column_part)

    for dest, (chosen, value) in sends.items():
        if dest[0] == "ahead":
            arrived = shift(value, "dev", dest[1])
        elif dest[0] == "behind":
            arrived = shift(value, "dev", -dest[1], cyclic=True)
        else:
            arrived = shift(value, "dev", -stride, cyclic=True)
        best = best.at[chosen[0] * width:(chosen[-1] + 1) * width].max(arrived)
    return best - 2.0


def solution(mesh):
    return jax.shard_map(
        body,
        mesh=mesh,
        in_specs=(P(("group", "dev"), None), P(("group", "dev"))),
        out_specs=P(("group", "dev")),
        check_vma=False,
    )
```

```python
import jax
import jax.numpy as jnp
from jax import lax
from jax.sharding import PartitionSpec as P


def shift(value, axis, steps, cyclic=False):
    count = lax.axis_size(axis)
    if cyclic:
        pairs = [(source, (source + steps) % count) for source in range(count)]
    else:
        pairs = [(source, source + steps) for source in range(max(0, -steps), min(count, count - steps))]
    return lax.ppermute(value, axis, pairs)


def unit_rows(embeddings):
    values_f = embeddings.astype(jnp.float32)
    squares = jnp.sum(values_f * values_f, axis=1, keepdims=True)
    return (values_f * lax.rsqrt(squares + 1e-06)).astype(jnp.bfloat16)


def body(embeddings, cluster_ids):
    rows, dim = embeddings.shape
    blocks = cluster_ids.shape[0]
    width = rows // blocks
    half = blocks // 2
    count = lax.axis_size("dev")
    stride = count // 4
    place = lax.axis_index("dev")
    first_block = (lax.axis_index("group") * count + place) * blocks
    unit = unit_rows(embeddings)

    own_tags = jnp.repeat(cluster_ids, width)
    local = jnp.arange(rows, dtype=jnp.int32)
    scores = jnp.dot(unit, unit.T, preferred_element_type=jnp.float32)
    keep = (own_tags[:, None] == own_tags[None, :]) & (local[:, None] != local[None, :])
    best = jnp.max(jnp.where(keep, scores + 2.0, jnp.zeros_like(scores)), axis=1)

    lag = first_block + jnp.arange(blocks, dtype=jnp.int32) - cluster_ids
    meta = jnp.zeros((16, dim), jnp.bfloat16).at[0, :blocks].set(lag.astype(jnp.bfloat16))
    extra = meta.shape[0]
    packet = jnp.concatenate([unit, meta], axis=0)
    everything = tuple(range(blocks))
    low, high = everything[:half], everything[half:]

    def part(pk, chosen):
        return jnp.concatenate([pk[chosen[0] * width:(chosen[-1] + 1) * width], pk[-extra:]], axis=0)

    def tile(a, a_blocks, b, b_blocks, k, valid):
        nb = len(b_blocks)
        lags = b[nb * width, b_blocks[0]:b_blocks[-1] + 1].astype(jnp.int32)
        block_reach = k * blocks + jnp.array(b_blocks, jnp.int32) - lags
        a_rows = jnp.concatenate([
            jnp.repeat(jnp.array(a_blocks, jnp.int32), width),
            jnp.full((a.shape[0] - len(a_blocks) * width,), -4 * rows, jnp.int32)])
        b_rows = jnp.concatenate([
            jnp.repeat(block_reach, width),
            jnp.full((b.shape[0] - nb * width,), 4 * rows, jnp.int32)])
        matched = (jnp.min(block_reach) <= max(a_blocks)) & valid

        def compute(unused):
            sims = jnp.dot(a, b.T, preferred_element_type=jnp.float32)
            same = b_rows[None, :] <= a_rows[:, None]
            shifted = jnp.where(same, sims + 2.0, jnp.zeros_like(sims))
            return (jnp.max(shifted, axis=1)[: len(a_blocks) * width],
                    jnp.max(shifted, axis=0)[: nb * width])

        def skipped(unused):
            return (jnp.zeros((len(a_blocks) * width,), jnp.float32),
                    jnp.zeros((nb * width,), jnp.float32))

        return lax.cond(matched, compute, skipped, 0)

    far_halves = [shift(unit[:half * width], "dev", stride, cyclic=True),
                  shift(unit[half * width:], "dev", stride, cyclic=True)]
    far = None
    far_ok = [(place >= stride) | (place < m) for m in range(4)]
    ahead = [packet]
    behind = [packet]
    def plan_of():
        return [
            (1, ("own",), everything, ("ahead", 1), everything, 1, True, ("best",), ("ahead", 1)),
            (1, ("behind", 1), everything, ("ahead", 1), everything, 2, place >= 1, ("behind", 1), ("ahead", 1)),
            (2, ("behind", 1), everything, ("ahead", 2), everything, 3, place >= 1, ("behind", 1), ("ahead", 2)),
            (2, ("behind", 2), everything, ("ahead", 2), everything, 4, place >= 2, ("behind", 2), ("ahead", 2)),
            (2, ("far",), everything, ("behind", 1), everything, stride - 1, far_ok[1], ("far",), ("behind", 1)),
            (2, ("far",), everything, ("behind", 2), everything, stride - 2, far_ok[2], ("far",), ("behind", 2)),
            (3, ("behind", 2), everything, ("ahead", 3), low, 5, place >= 2, ("behind", 2), ("ahead", 3)),
            (3, ("far",), everything, ("behind", 3), high, stride - 3, far_ok[3], ("far",), ("behind", 3)),
        ]

    def fetch(where):
        if where[0] == "own":
            return unit
        if where[0] == "far":
            return far
        return (ahead if where[0] == "ahead" else behind)[where[1]]

    sends = {}

    def gather(dest, chosen, value):
        nonlocal best
        if dest == ("best",):
            best = best.at[chosen[0] * width:(chosen[-1] + 1) * width].max(value)
        elif dest in sends:
            sends[dest] = (chosen, jnp.maximum(sends[dest][1], value))
        else:
            sends[dest] = (chosen, value)

    hops = 3
    plan = plan_of()
    for hop in range(1, hops + 1):
        if hop < hops:
            a_next = shift(ahead[-1], "dev", -1)
            b_next = shift(behind[-1], "dev", 1, cyclic=True)
        else:
            a_next = shift(part(ahead[-1], low), "dev", -1)
            b_next = shift(part(behind[-1], high), "dev", 1, cyclic=True)
        ready = [entry for entry in plan if entry[0] == hop - 1]
        pieces = [tile(fetch(e[1]), e[2], fetch(e[3]), e[4], e[5], e[6]) for e in ready]
        if hop == 1:
            a_next, b_next, first, best = lax.optimization_barrier((a_next, b_next, far_halves[0], best))
        elif hop == 2:
            a_next, b_next, second, pieces = lax.optimization_barrier((a_next, b_next, far_halves[1], pieces))
            far = jnp.concatenate([first, second], axis=0)
        else:
            a_next, b_next, pieces = lax.optimization_barrier((a_next, b_next, pieces))
        for e, (row_part, column_part) in zip(ready, pieces):
            gather(e[7], e[2], row_part)
            gather(e[8], e[4], column_part)
        ahead.append(a_next)
        behind.append(b_next)
    ready = [entry for entry in plan if entry[0] == hops]
    for e in ready:
        row_part, column_part = tile(fetch(e[1]), e[2], fetch(e[3]), e[4], e[5], e[6])
        gather(e[7], e[2], row_part)
        gather(e[8], e[4], column_part)

    for dest, (chosen, value) in sends.items():
        if dest[0] == "ahead":
            arrived = shift(value, "dev", dest[1])
        elif dest[0] == "behind":
            arrived = shift(value, "dev", -dest[1], cyclic=True)
        else:
            arrived = shift(value, "dev", -stride, cyclic=True)
        best = best.at[chosen[0] * width:(chosen[-1] + 1) * width].max(arrived)
    return best - 2.0


def solution(mesh):
    return jax.shard_map(
        body,
        mesh=mesh,
        in_specs=(P(("group", "dev"), None), P(("group", "dev"))),
        out_specs=P(("group", "dev")),
        check_vma=False,
    )
```

```python
import jax
import jax.numpy as jnp
from jax import lax
from jax.sharding import PartitionSpec as P


def shift(value, axis, steps, cyclic=False):
    count = lax.axis_size(axis)
    if cyclic:
        pairs = [(source, (source + steps) % count) for source in range(count)]
    else:
        pairs = [(source, source + steps) for source in range(max(0, -steps), min(count, count - steps))]
    return lax.ppermute(value, axis, pairs)


def unit_rows(embeddings):
    values_f = embeddings.astype(jnp.float32)
    squares = jnp.sum(values_f * values_f, axis=1, keepdims=True)
    return (values_f * lax.rsqrt(squares + 1e-06)).astype(jnp.bfloat16)


def body(embeddings, cluster_ids):
    rows, dim = embeddings.shape
    blocks = cluster_ids.shape[0]
    width = rows // blocks
    half = blocks // 2
    count = lax.axis_size("dev")
    stride = count // 4
    place = lax.axis_index("dev")
    first_block = (lax.axis_index("group") * count + place) * blocks
    unit = unit_rows(embeddings)

    own_tags = jnp.repeat(cluster_ids, width)
    local = jnp.arange(rows, dtype=jnp.int32)
    scores = jnp.dot(unit, unit.T, preferred_element_type=jnp.float32)
    keep = (own_tags[:, None] == own_tags[None, :]) & (local[:, None] != local[None, :])
    best = jnp.max(jnp.where(keep, scores + 2.0, jnp.zeros_like(scores)), axis=1)

    lag = first_block + jnp.arange(blocks, dtype=jnp.int32) - cluster_ids
    meta = jnp.zeros((16, dim), jnp.bfloat16).at[0, :blocks].set(lag.astype(jnp.bfloat16))
    extra = meta.shape[0]
    packet = jnp.concatenate([unit, meta], axis=0)
    everything = tuple(range(blocks))
    low, high = everything[:half], everything[half:]

    def part(pk, chosen):
        return jnp.concatenate([pk[chosen[0] * width:(chosen[-1] + 1) * width], pk[-extra:]], axis=0)

    def tile(a, a_blocks, b, b_blocks, k, valid):
        nb = len(b_blocks)
        lags = b[nb * width, b_blocks[0]:b_blocks[-1] + 1].astype(jnp.int32)
        block_reach = k * blocks + jnp.array(b_blocks, jnp.int32) - lags
        a_rows = jnp.concatenate([
            jnp.repeat(jnp.array(a_blocks, jnp.int32), width),
            jnp.full((a.shape[0] - len(a_blocks) * width,), -4 * rows, jnp.int32)])
        b_rows = jnp.concatenate([
            jnp.repeat(block_reach, width),
            jnp.full((b.shape[0] - nb * width,), 4 * rows, jnp.int32)])
        matched = (jnp.min(block_reach) <= max(a_blocks)) & valid

        def compute(unused):
            sims = jnp.dot(a, b.T, preferred_element_type=jnp.float32)
            same = b_rows[None, :] <= a_rows[:, None]
            shifted = jnp.where(same, sims + 2.0, jnp.zeros_like(sims))
            return (jnp.max(shifted, axis=1)[: len(a_blocks) * width],
                    jnp.max(shifted, axis=0)[: nb * width])

        def skipped(unused):
            return (jnp.zeros((len(a_blocks) * width,), jnp.float32),
                    jnp.zeros((nb * width,), jnp.float32))

        return lax.cond(matched, compute, skipped, 0)

    far_halves = [shift(unit[:half * width], "dev", stride, cyclic=True),
                  shift(unit[half * width:], "dev", stride, cyclic=True)]
    far = None
    far_ok = [(place >= stride) | (place < m) for m in range(4)]
    ahead = [packet]
    behind = [packet]
    def plan_of():
        return [
            (1, ("own",), everything, ("ahead", 1), everything, 1, True, ("best",), ("ahead", 1)),
            (1, ("behind", 1), everything, ("ahead", 1), everything, 2, place >= 1, ("behind", 1), ("ahead", 1)),
            (2, ("behind", 1), everything, ("ahead", 2), everything, 3, place >= 1, ("behind", 1), ("ahead", 2)),
            (2, ("behind", 2), everything, ("ahead", 2), everything, 4, place >= 2, ("behind", 2), ("ahead", 2)),
            (2, ("far",), everything, ("behind", 1), everything, stride - 1, far_ok[1], ("far",), ("behind", 1)),
            (2, ("far",), everything, ("behind", 2), everything, stride - 2, far_ok[2], ("far",), ("behind", 2)),
            (3, ("behind", 2), everything, ("ahead", 3), low, 5, place >= 2, ("behind", 2), ("ahead", 3)),
            (3, ("far",), everything, ("behind", 3), high, stride - 3, far_ok[3], ("far",), ("behind", 3)),
        ]

    def fetch(where):
        if where[0] == "own":
            return unit
        if where[0] == "far":
            return far
        return (ahead if where[0] == "ahead" else behind)[where[1]]

    sends = {}

    def gather(dest, chosen, value):
        nonlocal best
        if dest == ("best",):
            best = best.at[chosen[0] * width:(chosen[-1] + 1) * width].max(value)
        elif dest in sends:
            sends[dest] = (chosen, jnp.maximum(sends[dest][1], value))
        else:
            sends[dest] = (chosen, value)

    hops = 3
    plan = plan_of()
    sent_ahead, sent_behind = packet, packet
    for hop in range(1, hops + 1):
        if hop < hops:
            sent_ahead = shift(sent_ahead, "dev", -1)
            sent_behind = shift(sent_behind, "dev", 1, cyclic=True)
        else:
            sent_ahead = shift(part(sent_ahead, low), "dev", -1)
            sent_behind = shift(part(sent_behind, high), "dev", 1, cyclic=True)
        ready = [entry for entry in plan if entry[0] == hop - 1]
        pieces = [tile(fetch(e[1]), e[2], fetch(e[3]), e[4], e[5], e[6]) for e in ready]
        if hop == 1:
            a_next, b_next, first, best = lax.optimization_barrier((sent_ahead, sent_behind, far_halves[0], best))
        elif hop == 2:
            a_next, b_next, second, pieces = lax.optimization_barrier((sent_ahead, sent_behind, far_halves[1], pieces))
            far = jnp.concatenate([first, second], axis=0)
        else:
            a_next, b_next, pieces = lax.optimization_barrier((sent_ahead, sent_behind, pieces))
        for e, (row_part, column_part) in zip(ready, pieces):
            gather(e[7], e[2], row_part)
            gather(e[8], e[4], column_part)
        ahead.append(a_next)
        behind.append(b_next)
    ready = [entry for entry in plan if entry[0] == hops]
    for e in ready:
        row_part, column_part = tile(fetch(e[1]), e[2], fetch(e[3]), e[4], e[5], e[6])
        gather(e[7], e[2], row_part)
        gather(e[8], e[4], column_part)

    for dest, (chosen, value) in sends.items():
        if dest[0] == "ahead":
            arrived = shift(value, "dev", dest[1])
        elif dest[0] == "behind":
            arrived = shift(value, "dev", -dest[1], cyclic=True)
        else:
            arrived = shift(value, "dev", -stride, cyclic=True)
        best = best.at[chosen[0] * width:(chosen[-1] + 1) * width].max(arrived)
    return best - 2.0


def solution(mesh):
    return jax.shard_map(
        body,
        mesh=mesh,
        in_specs=(P(("group", "dev"), None), P(("group", "dev"))),
        out_specs=P(("group", "dev")),
        check_vma=False,
    )
```

```python
import jax
import jax.numpy as jnp
from jax import lax
from jax.sharding import PartitionSpec as P


def shift(value, axis, steps, cyclic=False):
    count = lax.axis_size(axis)
    if cyclic:
        pairs = [(source, (source + steps) % count) for source in range(count)]
    else:
        pairs = [(source, source + steps) for source in range(max(0, -steps), min(count, count - steps))]
    return lax.ppermute(value, axis, pairs)


def unit_rows(embeddings):
    values_f = embeddings.astype(jnp.float32)
    squares = jnp.sum(values_f * values_f, axis=1, keepdims=True)
    return (values_f * lax.rsqrt(squares + 1e-06)).astype(jnp.bfloat16)


def body(embeddings, cluster_ids):
    rows, dim = embeddings.shape
    blocks = cluster_ids.shape[0]
    width = rows // blocks
    half = blocks // 2
    count = lax.axis_size("dev")
    stride = count // 4
    place = lax.axis_index("dev")
    first_block = (lax.axis_index("group") * count + place) * blocks
    unit = unit_rows(embeddings)

    own_tags = jnp.repeat(cluster_ids, width)
    local = jnp.arange(rows, dtype=jnp.int32)
    scores = jnp.dot(unit, unit.T, preferred_element_type=jnp.float32)
    keep = (own_tags[:, None] == own_tags[None, :]) & (local[:, None] != local[None, :])
    best = jnp.max(jnp.where(keep, scores + 2.0, jnp.zeros_like(scores)), axis=1)

    lag = first_block + jnp.arange(blocks, dtype=jnp.int32) - cluster_ids
    meta = jnp.zeros((16, dim), jnp.bfloat16).at[0, :blocks].set(lag.astype(jnp.bfloat16))
    extra = meta.shape[0]
    packet = jnp.concatenate([unit, meta], axis=0)
    everything = tuple(range(blocks))
    low, high = everything[:half], everything[half:]

    def part(pk, chosen):
        return jnp.concatenate([pk[chosen[0] * width:(chosen[-1] + 1) * width], pk[-extra:]], axis=0)

    def tile(a, a_blocks, b, b_blocks, k, valid):
        nb = len(b_blocks)
        lags = b[nb * width, b_blocks[0]:b_blocks[-1] + 1].astype(jnp.int32)
        block_reach = k * blocks + jnp.array(b_blocks, jnp.int32) - lags
        a_rows = jnp.concatenate([
            jnp.repeat(jnp.array(a_blocks, jnp.int32), width),
            jnp.full((a.shape[0] - len(a_blocks) * width,), -4 * rows, jnp.int32)])
        b_rows = jnp.concatenate([
            jnp.repeat(block_reach, width),
            jnp.full((b.shape[0] - nb * width,), 4 * rows, jnp.int32)])
        matched = (jnp.min(block_reach) <= max(a_blocks)) & valid

        def compute(unused):
            sims = jnp.dot(a, b.T, preferred_element_type=jnp.float32)
            same = b_rows[None, :] <= a_rows[:, None]
            shifted = jnp.where(same, sims + 2.0, jnp.zeros_like(sims))
            return (jnp.max(shifted, axis=1)[: len(a_blocks) * width],
                    jnp.max(shifted, axis=0)[: nb * width])

        def skipped(unused):
            return (jnp.zeros((len(a_blocks) * width,), jnp.float32),
                    jnp.zeros((nb * width,), jnp.float32))

        return lax.cond(matched, compute, skipped, 0)

    far = shift(unit, "dev", stride, cyclic=True)
    far_ok = [(place >= stride) | (place < m) for m in range(4)]
    ahead = [packet]
    behind = [packet]
    def plan_of():
        return [
            (1, ("own",), everything, ("ahead", 1), everything, 1, True, ("best",), ("ahead", 1)),
            (1, ("behind", 1), everything, ("ahead", 1), everything, 2, place >= 1, ("behind", 1), ("ahead", 1)),
            (1, ("far",), everything, ("behind", 1), everything, stride - 1, far_ok[1], ("far",), ("behind", 1)),
            (2, ("behind", 1), everything, ("ahead", 2), everything, 3, place >= 1, ("behind", 1), ("ahead", 2)),
            (2, ("behind", 2), everything, ("ahead", 2), everything, 4, place >= 2, ("behind", 2), ("ahead", 2)),
            (2, ("far",), everything, ("behind", 2), everything, stride - 2, far_ok[2], ("far",), ("behind", 2)),
            (3, ("behind", 2), everything, ("ahead", 3), low, 5, place >= 2, ("behind", 2), ("ahead", 3)),
            (3, ("far",), everything, ("behind", 3), high, stride - 3, far_ok[3], ("far",), ("behind", 3)),
        ]

    def fetch(where):
        if where[0] == "own":
            return unit
        if where[0] == "far":
            return far
        return (ahead if where[0] == "ahead" else behind)[where[1]]

    sends = {}

    def gather(dest, chosen, value):
        nonlocal best
        if dest == ("best",):
            best = best.at[chosen[0] * width:(chosen[-1] + 1) * width].max(value)
        elif dest in sends:
            sends[dest] = (chosen, jnp.maximum(sends[dest][1], value))
        else:
            sends[dest] = (chosen, value)

    hops = 3
    plan = plan_of()
    for hop in range(1, hops + 1):
        if hop == 1:
            a_next = shift(packet, "dev", -1)
            b_next = shift(packet, "dev", 1, cyclic=True)
            first_ahead, first_behind = a_next, b_next
        elif hop < hops:
            source_a = first_ahead if hop == 2 else ahead[-1]
            source_b = first_behind if hop == 2 else behind[-1]
            a_next = shift(source_a, "dev", -1)
            b_next = shift(source_b, "dev", 1, cyclic=True)
        else:
            a_next = shift(part(ahead[-1], low), "dev", -1)
            b_next = shift(part(behind[-1], high), "dev", 1, cyclic=True)
        ready = [entry for entry in plan if entry[0] == hop - 1]
        pieces = [tile(fetch(e[1]), e[2], fetch(e[3]), e[4], e[5], e[6]) for e in ready]
        if hop == 1:
            a_next, b_next, far, best = lax.optimization_barrier((a_next, b_next, far, best))
        else:
            a_next, b_next, pieces = lax.optimization_barrier((a_next, b_next, pieces))
        for e, (row_part, column_part) in zip(ready, pieces):
            gather(e[7], e[2], row_part)
            gather(e[8], e[4], column_part)
        ahead.append(a_next)
        behind.append(b_next)
    ready = [entry for entry in plan if entry[0] == hops]
    for e in ready:
        row_part, column_part = tile(fetch(e[1]), e[2], fetch(e[3]), e[4], e[5], e[6])
        gather(e[7], e[2], row_part)
        gather(e[8], e[4], column_part)

    for dest, (chosen, value) in sends.items():
        if dest[0] == "ahead":
            arrived = shift(value, "dev", dest[1])
        elif dest[0] == "behind":
            arrived = shift(value, "dev", -dest[1], cyclic=True)
        else:
            arrived = shift(value, "dev", -stride, cyclic=True)
        best = best.at[chosen[0] * width:(chosen[-1] + 1) * width].max(arrived)
    return best - 2.0


def solution(mesh):
    return jax.shard_map(
        body,
        mesh=mesh,
        in_specs=(P(("group", "dev"), None), P(("group", "dev"))),
        out_specs=P(("group", "dev")),
        check_vma=False,
    )
```

```python
import jax
import jax.numpy as jnp
from jax import lax
from jax.sharding import PartitionSpec as P


def shift(value, axis, steps, cyclic=False):
    count = lax.axis_size(axis)
    if cyclic:
        pairs = [(source, (source + steps) % count) for source in range(count)]
    else:
        pairs = [(source, source + steps) for source in range(max(0, -steps), min(count, count - steps))]
    return lax.ppermute(value, axis, pairs)


def unit_rows(embeddings):
    values_f = embeddings.astype(jnp.float32)
    squares = jnp.sum(values_f * values_f, axis=1, keepdims=True)
    return (values_f * lax.rsqrt(squares + 1e-06)).astype(jnp.bfloat16)


def body(embeddings, cluster_ids):
    rows, dim = embeddings.shape
    blocks = cluster_ids.shape[0]
    width = rows // blocks
    half = blocks // 2
    count = lax.axis_size("dev")
    stride = count // 4
    place = lax.axis_index("dev")
    first_block = (lax.axis_index("group") * count + place) * blocks
    unit = unit_rows(embeddings)

    own_tags = jnp.repeat(cluster_ids, width)
    local = jnp.arange(rows, dtype=jnp.int32)
    scores = jnp.dot(unit, unit.T, preferred_element_type=jnp.float32)
    keep = (own_tags[:, None] == own_tags[None, :]) & (local[:, None] != local[None, :])
    best = jnp.max(jnp.where(keep, scores + 2.0, jnp.zeros_like(scores)), axis=1)

    lag = first_block + jnp.arange(blocks, dtype=jnp.int32) - cluster_ids
    meta = jnp.zeros((16, dim), jnp.bfloat16).at[0, :blocks].set(lag.astype(jnp.bfloat16))
    extra = meta.shape[0]
    packet = jnp.concatenate([unit, meta], axis=0)
    everything = tuple(range(blocks))
    low, high = everything[:half], everything[half:]

    def part(pk, chosen):
        return jnp.concatenate([pk[chosen[0] * width:(chosen[-1] + 1) * width], pk[-extra:]], axis=0)

    def tile(a, a_blocks, b, b_blocks, k, valid):
        nb = len(b_blocks)
        lags = b[nb * width, b_blocks[0]:b_blocks[-1] + 1].astype(jnp.int32)
        block_reach = k * blocks + jnp.array(b_blocks, jnp.int32) - lags
        a_rows = jnp.concatenate([
            jnp.repeat(jnp.array(a_blocks, jnp.int32), width),
            jnp.full((a.shape[0] - len(a_blocks) * width,), -4 * rows, jnp.int32)])
        b_rows = jnp.concatenate([
            jnp.repeat(block_reach, width),
            jnp.full((b.shape[0] - nb * width,), 4 * rows, jnp.int32)])
        matched = (jnp.min(block_reach) <= max(a_blocks)) & valid

        def compute(unused):
            sims = jnp.dot(a, b.T, preferred_element_type=jnp.float32)
            same = b_rows[None, :] <= a_rows[:, None]
            shifted = jnp.where(same, sims + 2.0, jnp.zeros_like(sims))
            return (jnp.max(shifted, axis=1)[: len(a_blocks) * width],
                    jnp.max(shifted, axis=0)[: nb * width])

        def skipped(unused):
            return (jnp.zeros((len(a_blocks) * width,), jnp.float32),
                    jnp.zeros((nb * width,), jnp.float32))

        return lax.cond(matched, compute, skipped, 0)

    far = jnp.concatenate([shift(unit[:half * width], "dev", stride, cyclic=True),
                           shift(unit[half * width:], "dev", stride, cyclic=True)], axis=0)
    far_ok = [(place >= stride) | (place < m) for m in range(4)]
    ahead = [packet]
    behind = [packet]
    def plan_of():
        return [
            (1, ("own",), everything, ("ahead", 1), everything, 1, True, ("best",), ("ahead", 1)),
            (1, ("behind", 1), everything, ("ahead", 1), everything, 2, place >= 1, ("behind", 1), ("ahead", 1)),
            (1, ("far",), everything, ("behind", 1), everything, stride - 1, far_ok[1], ("far",), ("behind", 1)),
            (2, ("behind", 1), everything, ("ahead", 2), everything, 3, place >= 1, ("behind", 1), ("ahead", 2)),
            (2, ("behind", 2), everything, ("ahead", 2), everything, 4, place >= 2, ("behind", 2), ("ahead", 2)),
            (2, ("far",), everything, ("behind", 2), everything, stride - 2, far_ok[2], ("far",), ("behind", 2)),
            (3, ("behind", 2), everything, ("ahead", 3), low, 5, place >= 2, ("behind", 2), ("ahead", 3)),
            (3, ("far",), everything, ("behind", 3), high, stride - 3, far_ok[3], ("far",), ("behind", 3)),
        ]

    def fetch(where):
        if where[0] == "own":
            return unit
        if where[0] == "far":
            return far
        return (ahead if where[0] == "ahead" else behind)[where[1]]

    sends = {}

    def gather(dest, chosen, value):
        nonlocal best
        if dest == ("best",):
            best = best.at[chosen[0] * width:(chosen[-1] + 1) * width].max(value)
        elif dest in sends:
            sends[dest] = (chosen, jnp.maximum(sends[dest][1], value))
        else:
            sends[dest] = (chosen, value)

    hops = 3
    plan = plan_of()
    for hop in range(1, hops + 1):
        if hop < hops:
            a_next = shift(ahead[-1], "dev", -1)
            b_next = shift(behind[-1], "dev", 1, cyclic=True)
        else:
            a_next = shift(part(ahead[-1], low), "dev", -1)
            b_next = shift(part(behind[-1], high), "dev", 1, cyclic=True)
        ready = [entry for entry in plan if entry[0] == hop - 1]
        pieces = [tile(fetch(e[1]), e[2], fetch(e[3]), e[4], e[5], e[6]) for e in ready]
        if hop == 1:
            a_next, b_next, far, best = lax.optimization_barrier((a_next, b_next, far, best))
        else:
            a_next, b_next, pieces = lax.optimization_barrier((a_next, b_next, pieces))
        for e, (row_part, column_part) in zip(ready, pieces):
            gather(e[7], e[2], row_part)
            gather(e[8], e[4], column_part)
        ahead.append(a_next)
        behind.append(b_next)
    ready = [entry for entry in plan if entry[0] == hops]
    for e in ready:
        row_part, column_part = tile(fetch(e[1]), e[2], fetch(e[3]), e[4], e[5], e[6])
        gather(e[7], e[2], row_part)
        gather(e[8], e[4], column_part)

    for dest, (chosen, value) in sends.items():
        if dest[0] == "ahead":
            arrived = shift(value, "dev", dest[1])
        elif dest[0] == "behind":
            arrived = shift(value, "dev", -dest[1], cyclic=True)
        else:
            arrived = shift(value, "dev", -stride, cyclic=True)
        best = best.at[chosen[0] * width:(chosen[-1] + 1) * width].max(arrived)
    return best - 2.0


def solution(mesh):
    return jax.shard_map(
        body,
        mesh=mesh,
        in_specs=(P(("group", "dev"), None), P(("group", "dev"))),
        out_specs=P(("group", "dev")),
        check_vma=False,
    )
```

```python
import jax
import jax.numpy as jnp
from jax import lax
from jax.sharding import PartitionSpec as P


def shift(value, axis, steps, cyclic=False):
    count = lax.axis_size(axis)
    if cyclic:
        pairs = [(source, (source + steps) % count) for source in range(count)]
    else:
        pairs = [(source, source + steps) for source in range(max(0, -steps), min(count, count - steps))]
    return lax.ppermute(value, axis, pairs)


def unit_rows(embeddings):
    values_f = embeddings.astype(jnp.float32)
    squares = jnp.sum(values_f * values_f, axis=1, keepdims=True)
    return (values_f * lax.rsqrt(squares + 1e-06)).astype(jnp.bfloat16)


def body(embeddings, cluster_ids):
    rows, dim = embeddings.shape
    blocks = cluster_ids.shape[0]
    width = rows // blocks
    half = blocks // 2
    count = lax.axis_size("dev")
    stride = count // 4
    place = lax.axis_index("dev")
    first_block = (lax.axis_index("group") * count + place) * blocks
    unit = unit_rows(embeddings)

    own_tags = jnp.repeat(cluster_ids, width)
    local = jnp.arange(rows, dtype=jnp.int32)
    scores = jnp.dot(unit, unit.T, preferred_element_type=jnp.float32)
    keep = (own_tags[:, None] == own_tags[None, :]) & (local[:, None] != local[None, :])
    best = jnp.max(jnp.where(keep, scores + 2.0, jnp.zeros_like(scores)), axis=1)

    lag = first_block + jnp.arange(blocks, dtype=jnp.int32) - cluster_ids
    meta = jnp.zeros((16, dim), jnp.bfloat16).at[0, :blocks].set(lag.astype(jnp.bfloat16))
    extra = meta.shape[0]
    packet = jnp.concatenate([unit, meta], axis=0)
    everything = tuple(range(blocks))
    low, high = everything[:half], everything[half:]

    def part(pk, chosen):
        return jnp.concatenate([pk[chosen[0] * width:(chosen[-1] + 1) * width], pk[-extra:]], axis=0)

    def tile(a, a_blocks, b, b_blocks, k, valid):
        nb = len(b_blocks)
        lags = b[nb * width, b_blocks[0]:b_blocks[-1] + 1].astype(jnp.int32)
        block_reach = k * blocks + jnp.array(b_blocks, jnp.int32) - lags
        a_rows = jnp.concatenate([
            jnp.repeat(jnp.array(a_blocks, jnp.int32), width),
            jnp.full((a.shape[0] - len(a_blocks) * width,), -4 * rows, jnp.int32)])
        b_rows = jnp.concatenate([
            jnp.repeat(block_reach, width),
            jnp.full((b.shape[0] - nb * width,), 4 * rows, jnp.int32)])
        matched = (jnp.min(block_reach) <= max(a_blocks)) & valid

        def compute(unused):
            sims = jnp.dot(a, b.T, preferred_element_type=jnp.float32)
            same = b_rows[None, :] <= a_rows[:, None]
            shifted = jnp.where(same, sims + 2.0, jnp.zeros_like(sims))
            return (jnp.max(shifted, axis=1)[: len(a_blocks) * width],
                    jnp.max(shifted, axis=0)[: nb * width])

        def skipped(unused):
            return (jnp.zeros((len(a_blocks) * width,), jnp.float32),
                    jnp.zeros((nb * width,), jnp.float32))

        return lax.cond(matched, compute, skipped, 0)

    far = jnp.concatenate([shift(unit[b * width:(b + 1) * width], "dev", stride, cyclic=True)
                           for b in everything], axis=0)
    far_ok = [(place >= stride) | (place < m) for m in range(4)]
    ahead = [packet]
    behind = [packet]
    def plan_of():
        return [
            (1, ("own",), everything, ("ahead", 1), everything, 1, True, ("best",), ("ahead", 1)),
            (1, ("behind", 1), everything, ("ahead", 1), everything, 2, place >= 1, ("behind", 1), ("ahead", 1)),
            (1, ("far",), everything, ("behind", 1), everything, stride - 1, far_ok[1], ("far",), ("behind", 1)),
            (2, ("behind", 1), everything, ("ahead", 2), everything, 3, place >= 1, ("behind", 1), ("ahead", 2)),
            (2, ("behind", 2), everything, ("ahead", 2), everything, 4, place >= 2, ("behind", 2), ("ahead", 2)),
            (2, ("far",), everything, ("behind", 2), everything, stride - 2, far_ok[2], ("far",), ("behind", 2)),
            (3, ("behind", 2), everything, ("ahead", 3), low, 5, place >= 2, ("behind", 2), ("ahead", 3)),
            (3, ("far",), everything, ("behind", 3), high, stride - 3, far_ok[3], ("far",), ("behind", 3)),
        ]

    def fetch(where):
        if where[0] == "own":
            return unit
        if where[0] == "far":
            return far
        return (ahead if where[0] == "ahead" else behind)[where[1]]

    sends = {}

    def gather(dest, chosen, value):
        nonlocal best
        if dest == ("best",):
            best = best.at[chosen[0] * width:(chosen[-1] + 1) * width].max(value)
        elif dest in sends:
            sends[dest] = (chosen, jnp.maximum(sends[dest][1], value))
        else:
            sends[dest] = (chosen, value)

    hops = 3
    plan = plan_of()
    for hop in range(1, hops + 1):
        if hop < hops:
            a_next = shift(ahead[-1], "dev", -1)
            b_next = shift(behind[-1], "dev", 1, cyclic=True)
        else:
            a_next = shift(part(ahead[-1], low), "dev", -1)
            b_next = shift(part(behind[-1], high), "dev", 1, cyclic=True)
        ready = [entry for entry in plan if entry[0] == hop - 1]
        pieces = [tile(fetch(e[1]), e[2], fetch(e[3]), e[4], e[5], e[6]) for e in ready]
        if hop == 1:
            a_next, b_next, far, best = lax.optimization_barrier((a_next, b_next, far, best))
        else:
            a_next, b_next, pieces = lax.optimization_barrier((a_next, b_next, pieces))
        for e, (row_part, column_part) in zip(ready, pieces):
            gather(e[7], e[2], row_part)
            gather(e[8], e[4], column_part)
        ahead.append(a_next)
        behind.append(b_next)
    ready = [entry for entry in plan if entry[0] == hops]
    for e in ready:
        row_part, column_part = tile(fetch(e[1]), e[2], fetch(e[3]), e[4], e[5], e[6])
        gather(e[7], e[2], row_part)
        gather(e[8], e[4], column_part)

    for dest, (chosen, value) in sends.items():
        if dest[0] == "ahead":
            arrived = shift(value, "dev", dest[1])
        elif dest[0] == "behind":
            arrived = shift(value, "dev", -dest[1], cyclic=True)
        else:
            arrived = shift(value, "dev", -stride, cyclic=True)
        best = best.at[chosen[0] * width:(chosen[-1] + 1) * width].max(arrived)
    return best - 2.0


def solution(mesh):
    return jax.shard_map(
        body,
        mesh=mesh,
        in_specs=(P(("group", "dev"), None), P(("group", "dev"))),
        out_specs=P(("group", "dev")),
        check_vma=False,
    )
```

```python
import jax
import jax.numpy as jnp
from jax import lax
from jax.sharding import PartitionSpec as P


def shift(value, axis, steps, cyclic=False):
    count = lax.axis_size(axis)
    if cyclic:
        pairs = [(source, (source + steps) % count) for source in range(count)]
    else:
        pairs = [(source, source + steps) for source in range(max(0, -steps), min(count, count - steps))]
    return lax.ppermute(value, axis, pairs)


def unit_rows(embeddings):
    values_f = embeddings.astype(jnp.float32)
    squares = jnp.sum(values_f * values_f, axis=1, keepdims=True)
    return (values_f * lax.rsqrt(squares + 1e-06)).astype(jnp.bfloat16)


def body(embeddings, cluster_ids):
    rows, dim = embeddings.shape
    blocks = cluster_ids.shape[0]
    width = rows // blocks
    half = blocks // 2
    count = lax.axis_size("dev")
    stride = count // 4
    place = lax.axis_index("dev")
    first_block = (lax.axis_index("group") * count + place) * blocks
    unit = unit_rows(embeddings)

    own_tags = jnp.repeat(cluster_ids, width)
    local = jnp.arange(rows, dtype=jnp.int32)
    scores = jnp.dot(unit, unit.T, preferred_element_type=jnp.float32)
    keep = (own_tags[:, None] == own_tags[None, :]) & (local[:, None] != local[None, :])
    best = jnp.max(jnp.where(keep, scores + 2.0, jnp.zeros_like(scores)), axis=1)

    lag = first_block + jnp.arange(blocks, dtype=jnp.int32) - cluster_ids
    meta = jnp.zeros((16, dim), jnp.bfloat16).at[0, :blocks].set(lag.astype(jnp.bfloat16))
    extra = meta.shape[0]
    packet = jnp.concatenate([unit, meta], axis=0)
    everything = tuple(range(blocks))
    low, high = everything[:half], everything[half:]

    def part(pk, chosen):
        return jnp.concatenate([pk[chosen[0] * width:(chosen[-1] + 1) * width], pk[-extra:]], axis=0)

    def tile(a, a_blocks, b, b_blocks, k, valid):
        nb = len(b_blocks)
        lags = b[nb * width, b_blocks[0]:b_blocks[-1] + 1].astype(jnp.int32)
        block_reach = k * blocks + jnp.array(b_blocks, jnp.int32) - lags
        a_rows = jnp.concatenate([
            jnp.repeat(jnp.array(a_blocks, jnp.int32), width),
            jnp.full((a.shape[0] - len(a_blocks) * width,), -4 * rows, jnp.int32)])
        b_rows = jnp.concatenate([
            jnp.repeat(block_reach, width),
            jnp.full((b.shape[0] - nb * width,), 4 * rows, jnp.int32)])
        matched = (jnp.min(block_reach) <= max(a_blocks)) & valid

        def compute(unused):
            sims = jnp.dot(a, b.T, preferred_element_type=jnp.float32)
            same = b_rows[None, :] <= a_rows[:, None]
            shifted = jnp.where(same, sims + 2.0, jnp.zeros_like(sims))
            return (jnp.max(shifted, axis=1)[: len(a_blocks) * width],
                    jnp.max(shifted, axis=0)[: nb * width])

        def skipped(unused):
            return (jnp.zeros((len(a_blocks) * width,), jnp.float32),
                    jnp.zeros((nb * width,), jnp.float32))

        return lax.cond(matched, compute, skipped, 0)

    far = jnp.concatenate([shift(unit[:half * width], "dev", stride, cyclic=True),
                           shift(unit[half * width:], "dev", stride, cyclic=True)], axis=0)
    far_ok = [(place >= stride) | (place < m) for m in range(4)]
    ahead = [packet]
    behind = [packet]
    def plan_of():
        return [
            (1, ("own",), everything, ("ahead", 1), everything, 1, True, ("best",), ("ahead", 1)),
            (1, ("behind", 1), everything, ("ahead", 1), everything, 2, place >= 1, ("behind", 1), ("ahead", 1)),
            (1, ("far",), everything, ("behind", 1), everything, stride - 1, far_ok[1], ("far",), ("behind", 1)),
            (2, ("behind", 1), everything, ("ahead", 2), everything, 3, place >= 1, ("behind", 1), ("ahead", 2)),
            (2, ("behind", 2), everything, ("ahead", 2), everything, 4, place >= 2, ("behind", 2), ("ahead", 2)),
            (2, ("far",), everything, ("behind", 2), everything, stride - 2, far_ok[2], ("far",), ("behind", 2)),
            (3, ("behind", 2), everything, ("ahead", 3), low, 5, place >= 2, ("behind", 2), ("ahead", 3)),
            (3, ("far",), everything, ("behind", 3), high, stride - 3, far_ok[3], ("far",), ("behind", 3)),
        ]

    def fetch(where):
        if where[0] == "own":
            return unit
        if where[0] == "far":
            return far
        return (ahead if where[0] == "ahead" else behind)[where[1]]

    sends = {}

    def gather(dest, chosen, value):
        nonlocal best
        if dest == ("best",):
            best = best.at[chosen[0] * width:(chosen[-1] + 1) * width].max(value)
        elif dest in sends:
            sends[dest] = (chosen, jnp.maximum(sends[dest][1], value))
        else:
            sends[dest] = (chosen, value)

    def deliver(dest, value):
        if dest[0] == "ahead":
            return shift(value, "dev", dest[1])
        if dest[0] == "behind":
            return shift(value, "dev", -dest[1], cyclic=True)
        return shift(value, "dev", -stride, cyclic=True)

    hops = 3
    plan = plan_of()
    last_dests = {e[7] for e in plan if e[0] == hops} | {e[8] for e in plan if e[0] == hops}
    for hop in range(1, hops + 1):
        if hop < hops:
            a_next = shift(ahead[-1], "dev", -1)
            b_next = shift(behind[-1], "dev", 1, cyclic=True)
        else:
            a_next = shift(part(ahead[-1], low), "dev", -1)
            b_next = shift(part(behind[-1], high), "dev", 1, cyclic=True)
        ready = [entry for entry in plan if entry[0] == hop - 1]
        pieces = [tile(fetch(e[1]), e[2], fetch(e[3]), e[4], e[5], e[6]) for e in ready]
        if hop == 1:
            a_next, b_next, far, best = lax.optimization_barrier((a_next, b_next, far, best))
        elif hop < hops:
            a_next, b_next, pieces = lax.optimization_barrier((a_next, b_next, pieces))
        else:
            for e, (row_part, column_part) in zip(ready, pieces):
                gather(e[7], e[2], row_part)
                gather(e[8], e[4], column_part)
            ready = []
            done = [dest for dest in sends if dest not in last_dests]
            arrivals = [deliver(dest, sends[dest][1]) for dest in done]
            kept = [dest for dest in sends if dest in last_dests]
            a_next, b_next, arrivals, held, best = lax.optimization_barrier(
                (a_next, b_next, arrivals, [sends[dest][1] for dest in kept], best))
            for dest, arrived in zip(done, arrivals):
                chosen = sends[dest][0]
                best = best.at[chosen[0] * width:(chosen[-1] + 1) * width].max(arrived)
            sends = {dest: (sends[dest][0], value) for dest, value in zip(kept, held)}
        for e, (row_part, column_part) in zip(ready, pieces):
            gather(e[7], e[2], row_part)
            gather(e[8], e[4], column_part)
        ahead.append(a_next)
        behind.append(b_next)
    ready = [entry for entry in plan if entry[0] == hops]
    for e in ready:
        row_part, column_part = tile(fetch(e[1]), e[2], fetch(e[3]), e[4], e[5], e[6])
        gather(e[7], e[2], row_part)
        gather(e[8], e[4], column_part)

    for dest, (chosen, value) in sends.items():
        best = best.at[chosen[0] * width:(chosen[-1] + 1) * width].max(deliver(dest, value))
    return best - 2.0


def solution(mesh):
    return jax.shard_map(
        body,
        mesh=mesh,
        in_specs=(P(("group", "dev"), None), P(("group", "dev"))),
        out_specs=P(("group", "dev")),
        check_vma=False,
    )
```

```python
import jax
import jax.numpy as jnp
from jax import lax
from jax.sharding import PartitionSpec as P


def shift(value, axis, steps, cyclic=False):
    count = lax.axis_size(axis)
    if cyclic:
        pairs = [(source, (source + steps) % count) for source in range(count)]
    else:
        pairs = [(source, source + steps) for source in range(max(0, -steps), min(count, count - steps))]
    return lax.ppermute(value, axis, pairs)


def unit_rows(embeddings):
    values_f = embeddings.astype(jnp.float32)
    squares = jnp.sum(values_f * values_f, axis=1, keepdims=True)
    return (values_f * lax.rsqrt(squares + 1e-06)).astype(jnp.bfloat16)


def body(embeddings, cluster_ids):
    rows, dim = embeddings.shape
    blocks = cluster_ids.shape[0]
    width = rows // blocks
    half = blocks // 2
    count = lax.axis_size("dev")
    stride = count // 4
    place = lax.axis_index("dev")
    first_block = (lax.axis_index("group") * count + place) * blocks
    unit = unit_rows(embeddings)

    own_tags = jnp.repeat(cluster_ids, width)
    local = jnp.arange(rows, dtype=jnp.int32)
    scores = jnp.dot(unit, unit.T, preferred_element_type=jnp.float32)
    keep = (own_tags[:, None] == own_tags[None, :]) & (local[:, None] != local[None, :])
    best = jnp.max(jnp.where(keep, scores + 2.0, jnp.zeros_like(scores)), axis=1)

    lag = first_block + jnp.arange(blocks, dtype=jnp.int32) - cluster_ids
    meta = jnp.zeros((16, dim), jnp.bfloat16).at[0, :blocks].set(lag.astype(jnp.bfloat16))
    extra = meta.shape[0]
    everything = tuple(range(blocks))
    low, high = everything[:half], everything[half:]
    packet = jnp.concatenate([unit[: half * width], meta, unit[half * width:]], axis=0)
    packet_layout = low + ("lags",) + high
    plain_layout = everything

    def length(segment):
        return extra if segment == "lags" else width

    def part(pk, chosen):
        if chosen == low:
            return pk[: half * width + extra], low + ("lags",)
        return pk[half * width:], ("lags",) + high

    def tile(a, a_layout, b, b_layout, k, valid):
        a_blocks = tuple(x for x in a_layout if x != "lags")
        b_blocks = tuple(x for x in b_layout if x != "lags")
        where = 0
        for segment in b_layout:
            if segment == "lags":
                break
            where += length(segment)
        lags = b[where, b_blocks[0]:b_blocks[-1] + 1].astype(jnp.int32)
        block_reach = k * blocks + jnp.array(b_blocks, jnp.int32) - lags
        a_rows = jnp.concatenate([
            jnp.full((extra,), -4 * rows, jnp.int32) if segment == "lags"
            else jnp.full((width,), segment, jnp.int32) for segment in a_layout])
        b_rows = jnp.concatenate([
            jnp.full((extra,), 4 * rows, jnp.int32) if segment == "lags"
            else jnp.full((width,), 0, jnp.int32) + block_reach[b_blocks.index(segment)]
            for segment in b_layout])
        matched = (jnp.min(block_reach) <= max(a_blocks)) & valid

        def drop_lags(values, layout):
            kept, start = [], 0
            for segment in layout:
                if segment != "lags":
                    kept.append(values[start:start + width])
                start += length(segment)
            return jnp.concatenate(kept)

        def compute(unused):
            sims = jnp.dot(a, b.T, preferred_element_type=jnp.float32)
            same = b_rows[None, :] <= a_rows[:, None]
            shifted = jnp.where(same, sims + 2.0, jnp.zeros_like(sims))
            return (drop_lags(jnp.max(shifted, axis=1), a_layout),
                    drop_lags(jnp.max(shifted, axis=0), b_layout))

        def skipped(unused):
            return (jnp.zeros((len(a_blocks) * width,), jnp.float32),
                    jnp.zeros((len(b_blocks) * width,), jnp.float32))

        return lax.cond(matched, compute, skipped, 0)

    far = jnp.concatenate([shift(unit[:half * width], "dev", stride, cyclic=True),
                           shift(unit[half * width:], "dev", stride, cyclic=True)], axis=0)
    far_ok = [(place >= stride) | (place < m) for m in range(4)]
    ahead = [(packet, packet_layout)]
    behind = [(packet, packet_layout)]
    def plan_of():
        return [
            (1, ("own",), everything, ("ahead", 1), everything, 1, True, ("best",), ("ahead", 1)),
            (1, ("behind", 1), everything, ("ahead", 1), everything, 2, place >= 1, ("behind", 1), ("ahead", 1)),
            (1, ("far",), everything, ("behind", 1), everything, stride - 1, far_ok[1], ("far",), ("behind", 1)),
            (2, ("behind", 1), everything, ("ahead", 2), everything, 3, place >= 1, ("behind", 1), ("ahead", 2)),
            (2, ("behind", 2), everything, ("ahead", 2), everything, 4, place >= 2, ("behind", 2), ("ahead", 2)),
            (2, ("far",), everything, ("behind", 2), everything, stride - 2, far_ok[2], ("far",), ("behind", 2)),
            (3, ("behind", 2), everything, ("ahead", 3), low, 5, place >= 2, ("behind", 2), ("ahead", 3)),
            (3, ("far",), everything, ("behind", 3), high, stride - 3, far_ok[3], ("far",), ("behind", 3)),
        ]

    def fetch(where):
        if where[0] == "own":
            return unit, plain_layout
        if where[0] == "far":
            return far, plain_layout
        return (ahead if where[0] == "ahead" else behind)[where[1]]

    sends = {}

    def gather(dest, chosen, value):
        nonlocal best
        if dest == ("best",):
            best = best.at[chosen[0] * width:(chosen[-1] + 1) * width].max(value)
        elif dest in sends:
            sends[dest] = (chosen, jnp.maximum(sends[dest][1], value))
        else:
            sends[dest] = (chosen, value)

    def deliver(dest, value):
        if dest[0] == "ahead":
            return shift(value, "dev", dest[1])
        if dest[0] == "behind":
            return shift(value, "dev", -dest[1], cyclic=True)
        return shift(value, "dev", -stride, cyclic=True)

    hops = 3
    plan = plan_of()
    last_dests = {e[7] for e in plan if e[0] == hops} | {e[8] for e in plan if e[0] == hops}
    for hop in range(1, hops + 1):
        if hop < hops:
            a_send, a_layout = ahead[-1]
            b_send, b_layout = behind[-1]
        else:
            a_send, a_layout = part(ahead[-1][0], low)
            b_send, b_layout = part(behind[-1][0], high)
        a_next = shift(a_send, "dev", -1)
        b_next = shift(b_send, "dev", 1, cyclic=True)
        ready = [entry for entry in plan if entry[0] == hop - 1]
        pieces = [tile(*fetch(e[1]), *fetch(e[3]), e[5], e[6]) for e in ready]
        if hop == 1:
            a_next, b_next, far, best = lax.optimization_barrier((a_next, b_next, far, best))
        elif hop < hops:
            a_next, b_next, pieces = lax.optimization_barrier((a_next, b_next, pieces))
        else:
            for e, (row_part, column_part) in zip(ready, pieces):
                gather(e[7], e[2], row_part)
                gather(e[8], e[4], column_part)
            ready = []
            done = [dest for dest in sends if dest not in last_dests]
            arrivals = [deliver(dest, sends[dest][1]) for dest in done]
            kept = [dest for dest in sends if dest in last_dests]
            a_next, b_next, arrivals, held, best = lax.optimization_barrier(
                (a_next, b_next, arrivals, [sends[dest][1] for dest in kept], best))
            for dest, arrived in zip(done, arrivals):
                chosen = sends[dest][0]
                best = best.at[chosen[0] * width:(chosen[-1] + 1) * width].max(arrived)
            sends = {dest: (sends[dest][0], value) for dest, value in zip(kept, held)}
        for e, (row_part, column_part) in zip(ready, pieces):
            gather(e[7], e[2], row_part)
            gather(e[8], e[4], column_part)
        ahead.append((a_next, a_layout))
        behind.append((b_next, b_layout))
    ready = [entry for entry in plan if entry[0] == hops]
    for e in ready:
        row_part, column_part = tile(*fetch(e[1]), *fetch(e[3]), e[5], e[6])
        gather(e[7], e[2], row_part)
        gather(e[8], e[4], column_part)

    for dest, (chosen, value) in sends.items():
        best = best.at[chosen[0] * width:(chosen[-1] + 1) * width].max(deliver(dest, value))
    return best - 2.0


def solution(mesh):
    return jax.shard_map(
        body,
        mesh=mesh,
        in_specs=(P(("group", "dev"), None), P(("group", "dev"))),
        out_specs=P(("group", "dev")),
        check_vma=False,
    )
```

```python
import jax
import jax.numpy as jnp
from jax import lax
from jax.sharding import PartitionSpec as P


def shift(value, axis, steps, cyclic=False):
    count = lax.axis_size(axis)
    if cyclic:
        pairs = [(source, (source + steps) % count) for source in range(count)]
    else:
        pairs = [(source, source + steps) for source in range(max(0, -steps), min(count, count - steps))]
    return lax.ppermute(value, axis, pairs)


def unit_rows(embeddings):
    values_f = embeddings.astype(jnp.float32)
    squares = jnp.sum(values_f * values_f, axis=1, keepdims=True)
    return (values_f * lax.rsqrt(squares + 1e-06)).astype(jnp.bfloat16)


def body(embeddings, cluster_ids):
    rows, dim = embeddings.shape
    blocks = cluster_ids.shape[0]
    width = rows // blocks
    half = blocks // 2
    count = lax.axis_size("dev")
    stride = count // 4
    place = lax.axis_index("dev")
    first_block = (lax.axis_index("group") * count + place) * blocks
    unit = unit_rows(embeddings)

    own_tags = jnp.repeat(cluster_ids, width)
    local = jnp.arange(rows, dtype=jnp.int32)
    scores = jnp.dot(unit, unit.T, preferred_element_type=jnp.float32)
    keep = (own_tags[:, None] == own_tags[None, :]) & (local[:, None] != local[None, :])
    best = jnp.max(jnp.where(keep, scores + 2.0, jnp.zeros_like(scores)), axis=1)

    lag = first_block + jnp.arange(blocks, dtype=jnp.int32) - cluster_ids
    meta = jnp.zeros((16, dim), jnp.bfloat16).at[0, :blocks].set(lag.astype(jnp.bfloat16))
    extra = meta.shape[0]
    packet = jnp.concatenate([unit, meta], axis=0)
    everything = tuple(range(blocks))
    low, high = everything[:half], everything[half:]

    def part(pk, chosen):
        return jnp.concatenate([pk[chosen[0] * width:(chosen[-1] + 1) * width], pk[-extra:]], axis=0)

    def tile(a, a_blocks, b, b_blocks, k, valid):
        nb = len(b_blocks)
        lags = b[nb * width, b_blocks[0]:b_blocks[-1] + 1].astype(jnp.int32)
        block_reach = k * blocks + jnp.array(b_blocks, jnp.int32) - lags
        a_rows = jnp.concatenate([
            jnp.repeat(jnp.array(a_blocks, jnp.int32), width),
            jnp.full((a.shape[0] - len(a_blocks) * width,), -4 * rows, jnp.int32)])
        b_rows = jnp.concatenate([
            jnp.repeat(block_reach, width),
            jnp.full((b.shape[0] - nb * width,), 4 * rows, jnp.int32)])
        matched = (jnp.min(block_reach) <= max(a_blocks)) & valid

        def compute(unused):
            sims = jnp.dot(a, b.T, preferred_element_type=jnp.float32)
            same = b_rows[None, :] <= a_rows[:, None]
            shifted = jnp.where(same, sims + 2.0, jnp.zeros_like(sims))
            return (jnp.max(shifted, axis=1)[: len(a_blocks) * width],
                    jnp.max(shifted, axis=0)[: nb * width])

        def skipped(unused):
            return (jnp.zeros((len(a_blocks) * width,), jnp.float32),
                    jnp.zeros((nb * width,), jnp.float32))

        return lax.cond(matched, compute, skipped, 0)

    far = jnp.concatenate([shift(unit[:half * width], "dev", stride, cyclic=True),
                           shift(unit[half * width:], "dev", stride, cyclic=True)], axis=0)
    far_ok = [(place >= stride) | (place < m) for m in range(4)]
    halves = (part(packet, low), part(packet, high))
    ahead = [halves]
    behind = [halves]
    joined = {}
    def plan_of():
        return [
            (1, ("own",), everything, ("ahead", 1), everything, 1, True, ("best",), ("ahead", 1)),
            (1, ("behind", 1), everything, ("ahead", 1), everything, 2, place >= 1, ("behind", 1), ("ahead", 1)),
            (1, ("far",), everything, ("behind", 1), everything, stride - 1, far_ok[1], ("far",), ("behind", 1)),
            (2, ("behind", 1), everything, ("ahead", 2), everything, 3, place >= 1, ("behind", 1), ("ahead", 2)),
            (2, ("behind", 2), everything, ("ahead", 2), everything, 4, place >= 2, ("behind", 2), ("ahead", 2)),
            (2, ("far",), everything, ("behind", 2), everything, stride - 2, far_ok[2], ("far",), ("behind", 2)),
            (3, ("behind", 2), everything, ("ahead", 3), low, 5, place >= 2, ("behind", 2), ("ahead", 3)),
            (3, ("far",), everything, ("behind", 3), high, stride - 3, far_ok[3], ("far",), ("behind", 3)),
        ]

    def fetch(where):
        if where[0] == "own":
            return unit
        if where[0] == "far":
            return far
        held = (ahead if where[0] == "ahead" else behind)[where[1]]
        if len(held) == 1:
            return held[0]
        if where not in joined:
            joined[where] = jnp.concatenate([held[0][: half * width], held[1]], axis=0)
        return joined[where]

    sends = {}

    def gather(dest, chosen, value):
        nonlocal best
        if dest == ("best",):
            best = best.at[chosen[0] * width:(chosen[-1] + 1) * width].max(value)
        elif dest in sends:
            sends[dest] = (chosen, jnp.maximum(sends[dest][1], value))
        else:
            sends[dest] = (chosen, value)

    def deliver(dest, value):
        if dest[0] == "ahead":
            return shift(value, "dev", dest[1])
        if dest[0] == "behind":
            return shift(value, "dev", -dest[1], cyclic=True)
        return shift(value, "dev", -stride, cyclic=True)

    hops = 3
    plan = plan_of()
    last_dests = {e[7] for e in plan if e[0] == hops} | {e[8] for e in plan if e[0] == hops}
    for hop in range(1, hops + 1):
        if hop < hops:
            a_next = tuple(shift(piece, "dev", -1) for piece in ahead[-1])
            b_next = tuple(shift(piece, "dev", 1, cyclic=True) for piece in behind[-1])
        else:
            a_next = (shift(ahead[-1][0], "dev", -1),)
            b_next = (shift(behind[-1][1], "dev", 1, cyclic=True),)
        ready = [entry for entry in plan if entry[0] == hop - 1]
        pieces = [tile(fetch(e[1]), e[2], fetch(e[3]), e[4], e[5], e[6]) for e in ready]
        if hop == 1:
            a_next, b_next, far, best = lax.optimization_barrier((a_next, b_next, far, best))
        elif hop < hops:
            a_next, b_next, pieces = lax.optimization_barrier((a_next, b_next, pieces))
        else:
            for e, (row_part, column_part) in zip(ready, pieces):
                gather(e[7], e[2], row_part)
                gather(e[8], e[4], column_part)
            ready = []
            done = [dest for dest in sends if dest not in last_dests]
            arrivals = [deliver(dest, sends[dest][1]) for dest in done]
            kept = [dest for dest in sends if dest in last_dests]
            a_next, b_next, arrivals, held, best = lax.optimization_barrier(
                (a_next, b_next, arrivals, [sends[dest][1] for dest in kept], best))
            for dest, arrived in zip(done, arrivals):
                chosen = sends[dest][0]
                best = best.at[chosen[0] * width:(chosen[-1] + 1) * width].max(arrived)
            sends = {dest: (sends[dest][0], value) for dest, value in zip(kept, held)}
        for e, (row_part, column_part) in zip(ready, pieces):
            gather(e[7], e[2], row_part)
            gather(e[8], e[4], column_part)
        ahead.append(a_next)
        behind.append(b_next)
    ready = [entry for entry in plan if entry[0] == hops]
    for e in ready:
        row_part, column_part = tile(fetch(e[1]), e[2], fetch(e[3]), e[4], e[5], e[6])
        gather(e[7], e[2], row_part)
        gather(e[8], e[4], column_part)

    for dest, (chosen, value) in sends.items():
        best = best.at[chosen[0] * width:(chosen[-1] + 1) * width].max(deliver(dest, value))
    return best - 2.0


def solution(mesh):
    return jax.shard_map(
        body,
        mesh=mesh,
        in_specs=(P(("group", "dev"), None), P(("group", "dev"))),
        out_specs=P(("group", "dev")),
        check_vma=False,
    )
```

```python
import jax
import jax.numpy as jnp
from jax import lax
from jax.sharding import PartitionSpec as P


def shift(value, axis, steps, cyclic=False):
    count = lax.axis_size(axis)
    if cyclic:
        pairs = [(source, (source + steps) % count) for source in range(count)]
    else:
        pairs = [(source, source + steps) for source in range(max(0, -steps), min(count, count - steps))]
    return lax.ppermute(value, axis, pairs)


def unit_rows(embeddings):
    values_f = embeddings.astype(jnp.float32)
    squares = jnp.sum(values_f * values_f, axis=1, keepdims=True)
    return (values_f * lax.rsqrt(squares + 1e-06)).astype(jnp.bfloat16)


def body(embeddings, cluster_ids):
    rows, dim = embeddings.shape
    blocks = cluster_ids.shape[0]
    width = rows // blocks
    half = blocks // 2
    count = lax.axis_size("dev")
    stride = count // 4
    place = lax.axis_index("dev")
    first_block = (lax.axis_index("group") * count + place) * blocks
    unit = unit_rows(embeddings)

    own_tags = jnp.repeat(cluster_ids, width)
    local = jnp.arange(rows, dtype=jnp.int32)
    scores = jnp.dot(unit, unit.T, preferred_element_type=jnp.float32)
    keep = (own_tags[:, None] == own_tags[None, :]) & (local[:, None] != local[None, :])
    best = jnp.max(jnp.where(keep, scores + 2.0, jnp.zeros_like(scores)), axis=1)

    lag = first_block + jnp.arange(blocks, dtype=jnp.int32) - cluster_ids
    meta = jnp.zeros((16, dim), jnp.bfloat16).at[0, :blocks].set(lag.astype(jnp.bfloat16))
    extra = meta.shape[0]
    packet = jnp.concatenate([unit, meta], axis=0)
    everything = tuple(range(blocks))
    low, high = everything[:half], everything[half:]

    def part(pk, chosen):
        return jnp.concatenate([pk[chosen[0] * width:(chosen[-1] + 1) * width], pk[-extra:]], axis=0)

    def tile(a, a_blocks, b, b_blocks, k, valid, guarded=True):
        nb = len(b_blocks)
        lags = b[nb * width, b_blocks[0]:b_blocks[-1] + 1].astype(jnp.int32)
        block_reach = k * blocks + jnp.array(b_blocks, jnp.int32) - lags
        a_rows = jnp.concatenate([
            jnp.repeat(jnp.array(a_blocks, jnp.int32), width),
            jnp.full((a.shape[0] - len(a_blocks) * width,), -4 * rows, jnp.int32)])
        b_rows = jnp.concatenate([
            jnp.repeat(block_reach, width),
            jnp.full((b.shape[0] - nb * width,), 4 * rows, jnp.int32)])
        matched = (jnp.min(block_reach) <= max(a_blocks)) & valid

        def compute(unused):
            sims = jnp.dot(a, b.T, preferred_element_type=jnp.float32)
            same = (b_rows[None, :] <= a_rows[:, None]) & valid
            shifted = jnp.where(same, sims + 2.0, jnp.zeros_like(sims))
            return (jnp.max(shifted, axis=1)[: len(a_blocks) * width],
                    jnp.max(shifted, axis=0)[: nb * width])

        def skipped(unused):
            return (jnp.zeros((len(a_blocks) * width,), jnp.float32),
                    jnp.zeros((nb * width,), jnp.float32))

        if not guarded:
            return compute(0)
        return lax.cond(matched, compute, skipped, 0)

    far = jnp.concatenate([shift(unit[:half * width], "dev", stride, cyclic=True),
                           shift(unit[half * width:], "dev", stride, cyclic=True)], axis=0)
    far_ok = [(place >= stride) | (place < m) for m in range(4)]
    ahead = [packet]
    behind = [packet]
    def plan_of():
        return [
            (1, ("own",), everything, ("ahead", 1), everything, 1, True, ("best",), ("ahead", 1)),
            (1, ("behind", 1), everything, ("ahead", 1), everything, 2, place >= 1, ("behind", 1), ("ahead", 1)),
            (1, ("far",), everything, ("behind", 1), everything, stride - 1, far_ok[1], ("far",), ("behind", 1)),
            (2, ("behind", 1), everything, ("ahead", 2), everything, 3, place >= 1, ("behind", 1), ("ahead", 2)),
            (2, ("behind", 2), everything, ("ahead", 2), everything, 4, place >= 2, ("behind", 2), ("ahead", 2)),
            (2, ("far",), everything, ("behind", 2), everything, stride - 2, far_ok[2], ("far",), ("behind", 2)),
            (3, ("behind", 2), everything, ("ahead", 3), low, 5, place >= 2, ("behind", 2), ("ahead", 3)),
            (3, ("far",), everything, ("behind", 3), high, stride - 3, far_ok[3], ("far",), ("behind", 3)),
        ]

    def fetch(where):
        if where[0] == "own":
            return unit
        if where[0] == "far":
            return far
        return (ahead if where[0] == "ahead" else behind)[where[1]]

    sends = {}

    def gather(dest, chosen, value):
        nonlocal best
        if dest == ("best",):
            best = best.at[chosen[0] * width:(chosen[-1] + 1) * width].max(value)
        elif dest in sends:
            sends[dest] = (chosen, jnp.maximum(sends[dest][1], value))
        else:
            sends[dest] = (chosen, value)

    def deliver(dest, value):
        if dest[0] == "ahead":
            return shift(value, "dev", dest[1])
        if dest[0] == "behind":
            return shift(value, "dev", -dest[1], cyclic=True)
        return shift(value, "dev", -stride, cyclic=True)

    hops = 3
    plan = plan_of()
    last_dests = {e[7] for e in plan if e[0] == hops} | {e[8] for e in plan if e[0] == hops}
    for hop in range(1, hops + 1):
        if hop < hops:
            a_next = shift(ahead[-1], "dev", -1)
            b_next = shift(behind[-1], "dev", 1, cyclic=True)
        else:
            a_next = shift(part(ahead[-1], low), "dev", -1)
            b_next = shift(part(behind[-1], high), "dev", 1, cyclic=True)
        ready = [entry for entry in plan if entry[0] == hop - 1]
        pieces = [tile(fetch(e[1]), e[2], fetch(e[3]), e[4], e[5], e[6]) for e in ready]
        if hop == 1:
            a_next, b_next, far, best = lax.optimization_barrier((a_next, b_next, far, best))
        elif hop < hops:
            a_next, b_next, pieces = lax.optimization_barrier((a_next, b_next, pieces))
        else:
            for e, (row_part, column_part) in zip(ready, pieces):
                gather(e[7], e[2], row_part)
                gather(e[8], e[4], column_part)
            ready = []
            done = [dest for dest in sends if dest not in last_dests]
            arrivals = [deliver(dest, sends[dest][1]) for dest in done]
            kept = [dest for dest in sends if dest in last_dests]
            a_next, b_next, arrivals, held, best = lax.optimization_barrier(
                (a_next, b_next, arrivals, [sends[dest][1] for dest in kept], best))
            for dest, arrived in zip(done, arrivals):
                chosen = sends[dest][0]
                best = best.at[chosen[0] * width:(chosen[-1] + 1) * width].max(arrived)
            sends = {dest: (sends[dest][0], value) for dest, value in zip(kept, held)}
        for e, (row_part, column_part) in zip(ready, pieces):
            gather(e[7], e[2], row_part)
            gather(e[8], e[4], column_part)
        ahead.append(a_next)
        behind.append(b_next)
    ready = [entry for entry in plan if entry[0] == hops]
    for e in ready:
        row_part, column_part = tile(fetch(e[1]), e[2], fetch(e[3]), e[4], e[5], e[6], guarded=False)
        gather(e[7], e[2], row_part)
        gather(e[8], e[4], column_part)

    for dest, (chosen, value) in sends.items():
        best = best.at[chosen[0] * width:(chosen[-1] + 1) * width].max(deliver(dest, value))
    return best - 2.0


def solution(mesh):
    return jax.shard_map(
        body,
        mesh=mesh,
        in_specs=(P(("group", "dev"), None), P(("group", "dev"))),
        out_specs=P(("group", "dev")),
        check_vma=False,
    )
```
